32 devices in a mesh: lay: 4 (over y, x), slab: 8 (over z, core).
Axes of the slice: x: 2, y: 2, z: 4, core: 2. Of those that a mesh axis runs over, the one named last changes fastest.
Arguments:
- cells: bfloat16 [16, 4, 64, 32, 128], P('slab', 'lay'), may hold values from -6 to 6
- noise: bfloat16 [16, 4, 64, 128], P('slab', 'lay'), may hold values from -6 to 6
- geometry: bfloat16 [4, 64, 128, 128], P('lay'), may hold values from -0.5 to 0.5
- tile_block: int32 [4, 64], P('lay'), may hold values from 0 to 31
- tile_count: int32 [4], P('lay'), may hold values from 1 to 64, 132 in all
- w_first: bfloat16 [3, 3, 3, 32, 32], replicated, may hold values from -0.21875 to 0.21875
- w_second: bfloat16 [3, 3, 3, 32, 32], replicated, may hold values from -0.21875 to 0.21875
- w_out: bfloat16 [32], replicated, may hold values from -1 to 1
Outputs:
- predicted: bfloat16 [16, 4, 64, 128], P('slab', 'lay')
- grad_first: float32 [3, 3, 3, 32, 32], replicated
- grad_second: float32 [3, 3, 3, 32, 32], replicated
- grad_out: float32 [32], replicated
The draws below stay inside these ranges and needn't reach their ends.
Inputs may be any that keep to these rules, and one draw needn't show every extreme that they name: `tile_count`: every layer has at least one live tile; the live tiles of all layers number 132, and some layer has exactly 64.
All inputs are finite; a program needn't handle non-finite values. No bound on the sum of `tile_count` on one device may be relied on, other than what follows from the above.
Results may differ from the reference program's by a relative error of at most 0.0095.
Values may be sent and summed in bfloat16 or wider, within the bound.
No kernel may reach another device: no remote copies, remote signals or barrier semaphores. Data moves between devices by JAX's collectives and lax.ppermute only.
A program may use at most 128 MiB of HBM per device.

```python
import math
import jax
import jax.numpy as jnp
import numpy as np
from jax import lax

CH = 32
GR = 64
GP = 64
TMAX = 64
LAYERS = 4
SHOWERS = 16
NBLK = 32
COUNTS_TOTAL = 132


def touch_ends(entries, rng, least, largest):
    spot = [jax.random.randint(jax.random.fold_in(rng, axis), (), 0, length) for axis, length in enumerate(entries.shape)]
    longest = entries.shape.index(max(entries.shape))
    neighbour = spot[:longest] + [(spot[longest] + 1) % entries.shape[longest]] + spot[longest + 1:]
    return entries.at[tuple(spot)].set(least).at[tuple(neighbour)].set(largest)


def levels(stream_key, shape, cuts, smallest, largest):
    level, own = 1.0, jax.random.fold_in(stream_key, 6)
    for position, shards_of in cuts:
        draws = jnp.exp(jax.random.uniform(jax.random.fold_in(own, position), (shards_of,), jnp.float32, smallest / len(cuts), largest / len(cuts)))
        level = level * jnp.repeat(draws, shape[position] // shards_of).reshape([-1 if axis == position else 1 for axis in range(len(shape))])
    return level


def profile(count, total, limit, slope):
    portions = [(1 << 20) // math.isqrt(grade ** slope) + 1 for grade in range(2, count + 1)]
    rest, holding = total - limit - (count - 1), [1] * (count - 1)
    while rest > 0:
        candidates = [i for i in range(count - 1) if holding[i] < limit]
        pool, remaining = sum([portions[i] for i in candidates]), rest
        for i in candidates:
            extra = min(limit - holding[i], max(1, remaining * portions[i] // pool), rest)
            holding[i] = holding[i] + extra
            rest = rest - extra
    return np.array([limit] + holding)


def uneven_parts(stream_key, number_of, total, limit, skew):
    if number_of == 2:
        one = jax.random.randint(stream_key, (), max(1, total - limit), min(limit, total - 1) + 1)
        return jnp.stack([one, total - one])
    sizes = jnp.asarray(profile(number_of, total, limit, skew), jnp.int32)
    couples = (number_of - 1) // 2
    giver, taker = sizes[1:1 + 2 * couples:2], sizes[2:2 + 2 * couples:2]
    margin = jnp.minimum(giver - 1, limit - taker)
    moved = jax.random.randint(jax.random.fold_in(stream_key, 1), (couples,), 0, 1 << 20) % (margin + 1)
    sizes = sizes.at[1:1 + 2 * couples:2].set(giver - moved).at[2:2 + 2 * couples:2].set(taker + moved)
    return sizes[jax.random.permutation(jax.random.fold_in(stream_key, 2), number_of)]


def gaussian(stream_key, shape, spread, most, split=(), kind=jnp.bfloat16):
    values = spread * jax.random.normal(stream_key, shape, jnp.float32)
    if split:
        values = values * levels(stream_key, shape, split, -0.22, 0.18)
    return jnp.clip(values, -most, most).astype(kind)


def setup_inputs(seed: int = 0) -> dict:
    key_list = jax.random.split(jax.random.key(seed), 9)
    return {
        "cells": gaussian(key_list[0], (SHOWERS, LAYERS, TMAX, CH, 128), 1.0, 6.0, ((0, 8), (1, 4))),
        "noise": gaussian(key_list[1], (SHOWERS, LAYERS, TMAX, 128), 1.0, 6.0, ((0, 8), (1, 4))),
        "geometry": gaussian(key_list[2], (LAYERS, TMAX, 128, 128), 128 ** -0.5, 0.5, ((0, 4),)),
        "tile_block": touch_ends(jax.random.randint(key_list[3], (LAYERS, TMAX), 0, NBLK), jax.random.fold_in(key_list[3], 1), 0, NBLK - 1).astype(jnp.int32),
        "tile_count": uneven_parts(key_list[4], LAYERS, COUNTS_TOTAL, TMAX, 2).astype(jnp.int32),
        "w_first": gaussian(key_list[5], (3, 3, 3, CH, CH), (27 * CH) ** -0.5, 0.21875),
        "w_second": gaussian(key_list[6], (3, 3, 3, CH, CH), (27 * CH) ** -0.5, 0.21875),
        "w_out": gaussian(key_list[7], (CH,), CH ** -0.5, 1.0),
    }


def shifted_taps(padded, offset_l, offset_r, layers, radial):
    window = padded[offset_l:offset_l + layers, offset_r:offset_r + radial]
    return jnp.concatenate([jnp.roll(window, 1 - offset_p, axis=2) for offset_p in range(3)], axis=3)


def conv_ref(field, weight):
    layers, radial = field.shape[0], field.shape[1]
    outputs = weight.shape[4]
    padded = jnp.pad(field, ((1, 1), (1, 1), (0, 0), (0, 0)))
    summed = jnp.zeros(field.shape[:3] + (outputs,), jnp.float32)
    for offset_l in range(3):
        for offset_r in range(3):
            stacked = shifted_taps(padded, offset_l, offset_r, layers, radial)
            summed = summed + jnp.einsum('lrpi,io->lrpo', stacked, weight[offset_l, offset_r].reshape(-1, outputs))
    return summed


def kernel_ref(field, gradient):
    layers, radial, channels = field.shape[0], field.shape[1], field.shape[3]
    padded = jnp.pad(field, ((1, 1), (1, 1), (0, 0), (0, 0)))
    parts = []
    for offset_l in range(3):
        for offset_r in range(3):
            stacked = shifted_taps(padded, offset_l, offset_r, layers, radial)
            parts.append(jnp.einsum('lrpi,lrpo->io', stacked, gradient).reshape(3, channels, gradient.shape[3]))
    return jnp.stack(parts).reshape(3, 3, 3, channels, gradient.shape[3])


def reference(cells, noise, geometry, tile_block, tile_count, w_first, w_second, w_out):
    live_mask = jnp.arange(TMAX)[None, :] < tile_count[:, None]
    route = (live_mask[:, :, None] & (tile_block[:, :, None] == jnp.arange(NBLK)[None, None, :])).astype(jnp.float32)
    live_f = live_mask.astype(jnp.float32)[:, :, None]
    geo_f = geometry.astype(jnp.float32)
    first_w = w_first.astype(jnp.float32)
    second_w = w_second.astype(jnp.float32)
    flipped = jnp.swapaxes(jnp.flip(second_w, (0, 1, 2)), 3, 4)
    out_weight = w_out.astype(jnp.float32)
    loss_scale = 32.0 / (SHOWERS * LAYERS * GR * GP)

    def per_shower(carry, inputs):
        cell_block, target = inputs
        mapped = jnp.einsum('ltcn,ltnp->ltcp', cell_block.astype(jnp.float32), geo_f)
        grid_map = jnp.einsum('ltcp,ltk->lkpc', mapped, route, precision=lax.Precision.HIGHEST)
        grid_map = grid_map.astype(jnp.bfloat16).reshape(LAYERS, GR, GP, CH)
        grid_f = grid_map.astype(jnp.float32)
        first = conv_ref(grid_f, first_w)
        active = jax.nn.silu(first).astype(jnp.bfloat16)
        mixed = grid_f + conv_ref(active.astype(jnp.float32), second_w)
        pred_grid = jnp.sum(mixed * out_weight, axis=-1).astype(jnp.bfloat16)
        picked = jnp.einsum('lkp,ltk->ltp', pred_grid.reshape(LAYERS, NBLK, 128).astype(jnp.float32), route)
        picked = picked.astype(jnp.bfloat16).astype(jnp.float32)
        predicted = jnp.einsum('ltp,ltnp->ltn', picked, geo_f).astype(jnp.bfloat16)
        cell_grad = ((predicted.astype(jnp.float32) - target.astype(jnp.float32)) * live_f * loss_scale).astype(jnp.bfloat16)
        back_map = jnp.einsum('ltn,ltnp->ltp', cell_grad.astype(jnp.float32), geo_f)
        grid_grad = jnp.einsum('ltp,ltk->lkp', back_map, route, precision=lax.Precision.HIGHEST)
        grid_grad = grid_grad.astype(jnp.bfloat16).reshape(LAYERS, GR, GP).astype(jnp.float32)
        grad_out = jnp.sum(mixed * grid_grad[..., None], axis=(0, 1, 2))
        second_grad = (grid_grad[..., None] * out_weight).astype(jnp.bfloat16).astype(jnp.float32)
        grad_second = kernel_ref(active.astype(jnp.float32), second_grad)
        active_grad = conv_ref(second_grad, flipped)
        sigmoid_z = jax.nn.sigmoid(first)
        first_grad = (active_grad * sigmoid_z * (1.0 + first * (1.0 - sigmoid_z))).astype(jnp.bfloat16)
        grad_first = kernel_ref(grid_f, first_grad.astype(jnp.float32))
        return (carry[0] + grad_first, carry[1] + grad_second, carry[2] + grad_out), predicted

    start = (jnp.zeros((3, 3, 3, CH, CH), jnp.float32), jnp.zeros((3, 3, 3, CH, CH), jnp.float32), jnp.zeros((CH,), jnp.float32))
    sums, predicted = lax.scan(per_shower, start, (cells, noise))
    return predicted, sums[0], sums[1], sums[2]
```

```python
import jax
import jax.numpy as jnp
from jax import lax
from jax.sharding import PartitionSpec as P

GR = 64
GP = 64

F32 = jnp.float32
BF16 = jnp.bfloat16


def layer_halo(x):
    count = lax.axis_size("lay")
    if count == 1:
        zeros = jnp.zeros_like(x[:, :1])
        return jnp.concatenate([zeros, x, zeros], axis=1)
    below = lax.ppermute(x[:, -1:], "lay", [(i, i + 1) for i in range(count - 1)])
    above = lax.ppermute(x[:, :1], "lay", [(i + 1, i) for i in range(count - 1)])
    return jnp.concatenate([below, x, above], axis=1)


def pad_rp(x):
    x = jnp.concatenate([x[..., -1:, :], x, x[..., :1, :]], axis=-2)
    pads = [(0, 0)] * (x.ndim - 3) + [(1, 1), (0, 0), (0, 0)]
    return jnp.pad(x, pads)


def conv3(xp, w):
    return lax.conv_general_dilated(
        xp, w, (1, 1, 1), "VALID",
        dimension_numbers=("NDHWC", "DHWIO", "NDHWC"),
        preferred_element_type=F32,
    )


def conv2(xp, w):
    return lax.conv_general_dilated(
        xp, w, (1, 1), "VALID",
        dimension_numbers=("NHWC", "HWIO", "NHWC"),
        preferred_element_type=F32,
    )


def wgrad3(xp, g):
    return lax.conv_general_dilated(
        xp, g, (1, 1, 1), "VALID",
        dimension_numbers=lax.ConvDimensionNumbers((4, 0, 1, 2, 3), (4, 0, 1, 2, 3), (3, 4, 0, 1, 2)),
        preferred_element_type=F32,
    )


def wgrad2(xp, g):
    return lax.conv_general_dilated(
        xp, g, (1, 1), "VALID",
        dimension_numbers=lax.ConvDimensionNumbers((3, 0, 1, 2), (3, 0, 1, 2), (2, 3, 0, 1)),
        preferred_element_type=F32,
    )


def per_device(cells, noise, geometry, tile_block, tile_count, w_first, w_second, w_out):
    showers, layer_count, tile_total, channels, cell_width = cells.shape
    block_total = GR * GP // 128
    slab_count = lax.axis_size("slab")
    lay_count = lax.axis_size("lay")
    live_mask = lax.broadcasted_iota(jnp.int32, (layer_count, tile_total), 1) < tile_count[:, None]
    block_ids = lax.broadcasted_iota(jnp.int32, (layer_count, tile_total, block_total), 2)
    onehot = (live_mask[:, :, None] & (tile_block[:, :, None] == block_ids)).astype(F32)
    out_weight = w_out.astype(F32)

    mapped = jnp.einsum("bltcn,ltnp->bltcp", cells, geometry, preferred_element_type=F32)
    grid_sum = jnp.einsum("bltcp,ltk->blkpc", mapped, onehot, precision=lax.Precision.HIGHEST)
    grid = grid_sum.astype(BF16).reshape(showers, layer_count, GR, GP, channels)

    grid_h = layer_halo(grid)
    grid_p = pad_rp(grid_h)
    first = conv3(grid_p, w_first)
    active = jax.nn.silu(first).astype(BF16)

    active_p = pad_rp(active).reshape(showers * layer_count, GR + 2, GP + 2, channels)
    stacked_w = jnp.transpose(w_second, (1, 2, 3, 0, 4)).reshape(3, 3, channels, 3 * channels)
    parts = conv2(active_p, stacked_w).reshape(showers, layer_count, GR, GP, 3, channels)
    projected = jnp.einsum("blrpio,o->iblrp", parts, out_weight, precision=lax.Precision.HIGHEST)
    lower = layer_halo(projected[0])[:, :layer_count]
    upper = layer_halo(projected[2])[:, 2:]
    grid_f = grid.astype(F32)
    own = jnp.einsum("blrpc,c->blrp", grid_f, out_weight, precision=lax.Precision.HIGHEST)
    pred_grid = (own + projected[1] + lower + upper).astype(BF16)

    block_grid = pred_grid.reshape(showers, layer_count, block_total, 128)
    picked = jnp.einsum(
        "blkp,ltk->bltp", block_grid, onehot.astype(BF16), preferred_element_type=F32
    ).astype(BF16)
    predicted = jnp.einsum(
        "bltp,ltnp->bltn", picked, geometry, preferred_element_type=F32
    ).astype(BF16)
    loss_scale = 32.0 / (showers * slab_count * layer_count * lay_count * GR * GP)
    live_f = live_mask.astype(F32)[None, :, :, None]
    cell_grad = (
        (predicted.astype(F32) - noise.astype(F32)) * live_f * loss_scale
    ).astype(BF16)
    back_map = jnp.einsum("bltn,ltnp->bltp", cell_grad, geometry, preferred_element_type=F32)
    grid_grad = jnp.einsum("bltp,ltk->blkp", back_map, onehot, precision=lax.Precision.HIGHEST)
    grid_grad = grid_grad.astype(BF16).reshape(showers, layer_count, GR, GP)

    grad_h = layer_halo(grid_grad).astype(F32)
    taps_grad = jnp.stack([grad_h[:, 2 - i : 2 - i + layer_count] for i in range(3)], axis=-1)
    grad_out = jnp.einsum("blrpc,blrp->c", grid_f, grad_h[:, 1 : 1 + layer_count],
                          precision=lax.Precision.HIGHEST)
    grad_out = grad_out + jnp.einsum("blrpio,blrpi->o", parts, taps_grad,
                                     precision=lax.Precision.HIGHEST)

    second_h = (grad_h[..., None] * out_weight).astype(BF16)
    taps_second = jnp.stack([second_h[:, 2 - i : 2 - i + layer_count] for i in range(3)], axis=-2)
    taps_second = taps_second.reshape(showers * layer_count, GR, GP, 3 * channels)
    grad_second = wgrad2(active_p, taps_second).reshape(3, 3, channels, 3, channels)
    grad_second = jnp.transpose(grad_second, (3, 0, 1, 2, 4))

    flipped = jnp.swapaxes(jnp.flip(w_second, (0, 1, 2)), 3, 4)
    active_grad = conv3(pad_rp(second_h), flipped)
    sigmoid_z = jax.nn.sigmoid(first)
    first_grad = (active_grad * sigmoid_z * (1.0 + first * (1.0 - sigmoid_z))).astype(BF16)
    grad_first = wgrad3(grid_p, first_grad)

    size = grad_first.size
    flat = jnp.concatenate([grad_first.reshape(-1), grad_second.reshape(-1), grad_out])
    flat = lax.psum(flat, ("lay", "slab"))
    grad_first = flat[:size].reshape(grad_first.shape)
    grad_second = flat[size : 2 * size].reshape(grad_first.shape)
    grad_out = flat[2 * size :]
    return (predicted, grad_first, grad_second, grad_out)


def solution(mesh):
    in_specs = (
        P("slab", "lay", None, None, None),
        P("slab", "lay", None, None),
        P("lay", None, None, None),
        P("lay", None),
        P("lay"),
        P(),
        P(),
        P(),
    )
    out_specs = (P("slab", "lay", None, None), P(), P(), P())
    return jax.shard_map(
        per_device, mesh=mesh, in_specs=in_specs, out_specs=out_specs, check_vma=False
    )
```

```python
import jax
import jax.numpy as jnp
from jax import lax
from jax.sharding import PartitionSpec as P

GR = 64
GP = 64
BLK = 8

F32 = jnp.float32
BF16 = jnp.bfloat16
HIGH = lax.Precision.HIGHEST


def layer_halo(x):
    count = lax.axis_size("lay")
    if count == 1:
        zeros = jnp.zeros_like(x[:, :1])
        return jnp.concatenate([zeros, x, zeros], axis=1)
    below = lax.ppermute(x[:, -1:], "lay", [(i, i + 1) for i in range(count - 1)])
    above = lax.ppermute(x[:, :1], "lay", [(i + 1, i) for i in range(count - 1)])
    return jnp.concatenate([below, x, above], axis=1)


def unfold(x):
    s, d, r, p, c = x.shape
    main = x.reshape(s, d, r, p // BLK, BLK * c)
    left = jnp.roll(main[..., (BLK - 1) * c :], 1, axis=3)
    right = jnp.roll(main[..., :c], -1, axis=3)
    full = jnp.concatenate([left, main, right], axis=-1)
    return jnp.pad(full, ((0, 0), (0, 0), (1, 1), (0, 0), (0, 0)))


def selector():
    shape = (3, BLK + 2, BLK)
    rows_idx = lax.broadcasted_iota(jnp.int32, shape, 1)
    cols_idx = lax.broadcasted_iota(jnp.int32, shape, 2)
    tap_idx = lax.broadcasted_iota(jnp.int32, shape, 0)
    return (rows_idx == cols_idx + tap_idx).astype(F32)


def banded(weight):
    c, o = weight.shape[3], weight.shape[4]
    matrix = jnp.einsum("mqp,ijmco->ijqcpo", selector(), weight.astype(F32), precision=HIGH)
    return matrix.reshape(3, 3, (BLK + 2) * c, BLK * o).astype(BF16)


def band_sum(product, c, o):
    lead = product.shape[:-2]
    product = product.reshape(lead + (BLK + 2, c, BLK, o))
    return jnp.einsum("mqp,...qipo->...mio", selector(), product, precision=HIGH)


def conv_layers(xu, matrices, layers):
    radial = xu.shape[2] - 2
    total = None
    for i in range(3):
        for j in range(3):
            term = jnp.einsum(
                "slrqk,kn->slrqn", xu[:, i : i + layers, j : j + radial], matrices[i, j],
                preferred_element_type=F32,
            )
            total = term if total is None else total + term
    return total


def tree_sum(x, axes):
    for axis in axes:
        size = lax.axis_size(axis)
        if size & (size - 1):
            x = lax.psum(x, axis)
            continue
        step = 1
        while step < size:
            x = x + lax.ppermute(x, axis, [(i, i ^ step) for i in range(size)])
            step *= 2
    return x


def per_device(cells, noise, geometry, tile_block, tile_count, w_first, w_second, w_out):
    showers, layer_count, tile_total, channels, cell_width = cells.shape
    block_total = GR * GP // 128
    slab_count = lax.axis_size("slab")
    lay_count = lax.axis_size("lay")
    nq = GP // BLK
    live_mask = lax.broadcasted_iota(jnp.int32, (layer_count, tile_total), 1) < tile_count[:, None]
    block_ids = lax.broadcasted_iota(jnp.int32, (layer_count, tile_total, block_total), 2)
    onehot = (live_mask[:, :, None] & (tile_block[:, :, None] == block_ids)).astype(F32)
    out_weight = w_out.astype(F32)

    mapped = jnp.einsum("bltcn,ltnp->bltcp", cells, geometry, preferred_element_type=F32)
    grid_sum = jnp.einsum("bltcp,ltk->blkpc", mapped, onehot, precision=HIGH)
    grid = grid_sum.astype(BF16).reshape(showers, layer_count, GR, GP, channels)

    grid_u = unfold(layer_halo(grid))
    first = conv_layers(grid_u, banded(w_first), layer_count)
    first = first.reshape(showers, layer_count, GR, GP, channels)
    active = jax.nn.silu(first).astype(BF16)

    active_u = unfold(active)
    second_band = banded(w_second)
    stacked = jnp.concatenate([second_band[i] for i in range(3)], axis=-1)
    parts = None
    for j in range(3):
        term = jnp.einsum(
            "slrqk,kn->slrqn", active_u[:, :, j : j + GR], stacked[j], preferred_element_type=F32
        )
        parts = term if parts is None else parts + term
    parts = parts.reshape(showers, layer_count, GR, nq, 3, BLK, channels)
    projected = jnp.einsum("blrqitc,c->iblrqt", parts, out_weight, precision=HIGH)
    projected = projected.reshape(3, showers, layer_count, GR, GP)
    lower = layer_halo(projected[0])[:, :layer_count]
    upper = layer_halo(projected[2])[:, 2:]
    grid_f = grid.astype(F32)
    own = jnp.einsum("blrpc,c->blrp", grid_f, out_weight, precision=HIGH)
    pred_grid = (own + projected[1] + lower + upper).astype(BF16)

    block_grid = pred_grid.reshape(showers, layer_count, block_total, 128)
    picked = jnp.einsum(
        "blkp,ltk->bltp", block_grid, onehot.astype(BF16), preferred_element_type=F32
    ).astype(BF16)
    predicted = jnp.einsum(
        "bltp,ltnp->bltn", picked, geometry, preferred_element_type=F32
    ).astype(BF16)
    loss_scale = 32.0 / (showers * slab_count * layer_count * lay_count * GR * GP)
    live_f = live_mask.astype(F32)[None, :, :, None]
    cell_grad = (
        (predicted.astype(F32) - noise.astype(F32)) * live_f * loss_scale
    ).astype(BF16)
    back_map = jnp.einsum("bltn,ltnp->bltp", cell_grad, geometry, preferred_element_type=F32)
    grid_grad = jnp.einsum("bltp,ltk->blkp", back_map, onehot, precision=HIGH)
    grid_grad = grid_grad.astype(BF16).reshape(showers, layer_count, GR, GP)

    grad_h = layer_halo(grid_grad).astype(F32)
    taps_grad = jnp.stack([grad_h[:, 2 - i : 2 - i + layer_count] for i in range(3)], axis=0)
    taps_grad = taps_grad.reshape(3, showers, layer_count, GR, nq, BLK)
    grad_out = jnp.einsum("blrpc,blrp->c", grid_f, grad_h[:, 1 : 1 + layer_count], precision=HIGH)
    grad_out = grad_out + jnp.einsum("blrqitc,iblrqt->c", parts, taps_grad, precision=HIGH)

    second_h = (grad_h[..., None] * out_weight).astype(BF16)
    width = BLK * channels
    taps_second = jnp.concatenate(
        [second_h[:, 2 - i : 2 - i + layer_count].reshape(showers, layer_count, GR, nq, width)
         for i in range(3)],
        axis=-1,
    )
    grad_second = []
    for j in range(3):
        product = jnp.einsum(
            "slrqk,slrqn->kn", active_u[:, :, j : j + GR], taps_second, preferred_element_type=F32
        )
        product = product.reshape(product.shape[0], 3, width)
        grad_second.append(jnp.stack([band_sum(product[:, i], channels, channels) for i in range(3)]))
    grad_second = jnp.stack(grad_second, axis=1)

    flipped = jnp.swapaxes(jnp.flip(w_second, (0, 1, 2)), 3, 4)
    active_grad = conv_layers(unfold(second_h), banded(flipped), layer_count)
    active_grad = active_grad.reshape(showers, layer_count, GR, GP, channels)
    sigmoid_z = jax.nn.sigmoid(first)
    first_grad = (active_grad * sigmoid_z * (1.0 + first * (1.0 - sigmoid_z))).astype(BF16)
    first_grad = first_grad.reshape(showers, layer_count, GR, nq, width)
    grad_first = []
    for i in range(3):
        for j in range(3):
            product = jnp.einsum(
                "slrqk,slrqn->kn", grid_u[:, i : i + layer_count, j : j + GR], first_grad,
                preferred_element_type=F32,
            )
            grad_first.append(band_sum(product, channels, channels))
    grad_first = jnp.stack(grad_first).reshape(3, 3, 3, channels, channels)

    size = grad_first.size
    flat = jnp.concatenate([grad_first.reshape(-1), grad_second.reshape(-1), grad_out])
    flat = tree_sum(flat, ("slab", "lay"))
    grad_first = flat[:size].reshape(grad_first.shape)
    grad_second = flat[size : 2 * size].reshape(grad_first.shape)
    grad_out = flat[2 * size :]
    return (predicted, grad_first, grad_second, grad_out)


def solution(mesh):
    in_specs = (
        P("slab", "lay", None, None, None),
        P("slab", "lay", None, None),
        P("lay", None, None, None),
        P("lay", None),
        P("lay"),
        P(),
        P(),
        P(),
    )
    out_specs = (P("slab", "lay", None, None), P(), P(), P())
    return jax.shard_map(
        per_device, mesh=mesh, in_specs=in_specs, out_specs=out_specs, check_vma=False
    )
```

```python
import jax
import jax.numpy as jnp
from jax import lax
from jax.sharding import PartitionSpec as P

GR = 64
GP = 64
BLK = 8

F32 = jnp.float32
BF16 = jnp.bfloat16
HIGH = lax.Precision.HIGHEST


def layer_halo(x):
    count = lax.axis_size("lay")
    if count == 1:
        zeros = jnp.zeros_like(x[:, :1])
        return jnp.concatenate([zeros, x, zeros], axis=1)
    below = lax.ppermute(x[:, -1:], "lay", [(i, i + 1) for i in range(count - 1)])
    above = lax.ppermute(x[:, :1], "lay", [(i + 1, i) for i in range(count - 1)])
    return jnp.concatenate([below, x, above], axis=1)


def unfold(x):
    s, d, r, p, c = x.shape
    main = x.reshape(s, d, r, p // BLK, BLK * c)
    left = jnp.roll(main[..., (BLK - 1) * c :], 1, axis=3)
    right = jnp.roll(main[..., :c], -1, axis=3)
    full = jnp.concatenate([left, main, right], axis=-1)
    return jnp.pad(full, ((0, 0), (0, 0), (1, 1), (0, 0), (0, 0)))


def selector():
    shape = (3, BLK + 2, BLK)
    rows_idx = lax.broadcasted_iota(jnp.int32, shape, 1)
    cols_idx = lax.broadcasted_iota(jnp.int32, shape, 2)
    tap_idx = lax.broadcasted_iota(jnp.int32, shape, 0)
    return (rows_idx == cols_idx + tap_idx).astype(F32)


def banded(weight):
    c, o = weight.shape[3], weight.shape[4]
    rows, cols = (BLK + 2) * c, BLK * o
    tap = (lax.broadcasted_iota(jnp.int32, (rows, cols), 0) // c
           - lax.broadcasted_iota(jnp.int32, (rows, cols), 1) // o)
    tiled = jnp.tile(weight, (1, 1, 1, BLK + 2, BLK))
    out = jnp.zeros((3, 3, rows, cols), weight.dtype)
    for m in range(3):
        out = jnp.where((tap == m)[None, None], tiled[:, :, m], out)
    return out


def columns(xu, layers, layer_taps):
    radial = xu.shape[2] - 2
    pieces = [xu[:, i : i + layers, j : j + radial] for i in range(layer_taps) for j in range(3)]
    x = jnp.concatenate(pieces, axis=-1)
    return x.reshape(-1, x.shape[-1])


def tree_sum(x, axes):
    for axis in axes:
        size = lax.axis_size(axis)
        if size & (size - 1):
            x = lax.psum(x, axis)
            continue
        step = 1
        while step < size:
            x = x + lax.ppermute(x, axis, [(i, i ^ step) for i in range(size)])
            step *= 2
    return x


def per_device(cells, noise, geometry, tile_block, tile_count, w_first, w_second, w_out):
    showers, layer_count, tile_total, channels, cell_width = cells.shape
    block_total = GR * GP // 128
    slab_count = lax.axis_size("slab")
    lay_count = lax.axis_size("lay")
    nq = GP // BLK
    live_mask = lax.broadcasted_iota(jnp.int32, (layer_count, tile_total), 1) < tile_count[:, None]
    block_ids = lax.broadcasted_iota(jnp.int32, (layer_count, tile_total, block_total), 2)
    onehot = (live_mask[:, :, None] & (tile_block[:, :, None] == block_ids)).astype(F32)
    out_weight = w_out.astype(F32)

    mapped = jnp.einsum("bltcn,ltnp->bltcp", cells, geometry, preferred_element_type=F32)
    grid_sum = jnp.einsum("bltcp,ltk->blkpc", mapped, onehot, precision=HIGH)
    grid = grid_sum.astype(BF16).reshape(showers, layer_count, GR, GP, channels)

    rows = showers * layer_count * GR * nq
    width = BLK * channels
    grid_x = columns(unfold(layer_halo(grid)), layer_count, 3)
    first = jnp.dot(grid_x, banded(w_first).reshape(-1, width), preferred_element_type=F32)
    first = first.reshape(showers, layer_count, GR, GP, channels)
    active = jax.nn.silu(first).astype(BF16)

    active_x = columns(unfold(active), layer_count, 1)
    second_band = jnp.transpose(banded(w_second), (1, 2, 0, 3))
    second_band = second_band.reshape(3 * second_band.shape[1], 3 * width)
    parts = jnp.dot(active_x, second_band, preferred_element_type=F32)
    lane = lax.broadcasted_iota(jnp.int32, (3 * width, 3 * BLK), 0)
    slot = lax.broadcasted_iota(jnp.int32, (3 * width, 3 * BLK), 1)
    project = jnp.where(lane // channels == slot, jnp.tile(out_weight, 3 * BLK)[:, None], 0.0)
    projected = jnp.dot(parts, project, precision=HIGH)
    projected = projected.reshape(showers, layer_count, GR, nq, 3, BLK)
    projected = jnp.transpose(projected, (4, 0, 1, 2, 3, 5)).reshape(3, showers, layer_count, GR, GP)
    lower = layer_halo(projected[0])[:, :layer_count]
    upper = layer_halo(projected[2])[:, 2:]
    grid_f = grid.astype(F32)
    own = jnp.einsum("blrpc,c->blrp", grid_f, out_weight, precision=HIGH)
    pred_grid = (own + projected[1] + lower + upper).astype(BF16)

    block_grid = pred_grid.reshape(showers, layer_count, block_total, 128)
    picked = jnp.einsum(
        "blkp,ltk->bltp", block_grid, onehot.astype(BF16), preferred_element_type=F32
    ).astype(BF16)
    predicted = jnp.einsum(
        "bltp,ltnp->bltn", picked, geometry, preferred_element_type=F32
    ).astype(BF16)
    loss_scale = 32.0 / (showers * slab_count * layer_count * lay_count * GR * GP)
    live_f = live_mask.astype(F32)[None, :, :, None]
    cell_grad = (
        (predicted.astype(F32) - noise.astype(F32)) * live_f * loss_scale
    ).astype(BF16)
    back_map = jnp.einsum("bltn,ltnp->bltp", cell_grad, geometry, preferred_element_type=F32)
    grid_grad = jnp.einsum("bltp,ltk->blkp", back_map, onehot, precision=HIGH)
    grid_grad = grid_grad.astype(BF16).reshape(showers, layer_count, GR, GP)

    grad_h = layer_halo(grid_grad).astype(F32)
    taps_grad = jnp.stack(
        [grad_h[:, 2 - i : 2 - i + layer_count].reshape(showers, layer_count, GR, nq, BLK)
         for i in range(3)],
        axis=4,
    ).reshape(rows, 3 * BLK)
    grad_out = jnp.einsum("blrpc,blrp->c", grid_f, grad_h[:, 1 : 1 + layer_count], precision=HIGH)
    weighted = parts.reshape(rows, 3 * BLK, channels) * taps_grad[:, :, None]
    grad_out = grad_out + jnp.sum(weighted, axis=(0, 1))

    second_h = (grad_h[..., None] * out_weight).astype(BF16)
    taps_second = jnp.concatenate(
        [second_h[:, 2 - i : 2 - i + layer_count].reshape(rows, width) for i in range(3)], axis=-1
    )
    product = lax.dot_general(
        taps_second, active_x, (((0,), (0,)), ((), ())), preferred_element_type=F32
    ).reshape(3, BLK, channels, 3, BLK + 2, channels)
    grad_second = jnp.einsum("mqp,ipojqc->ijmco", selector(), product, precision=HIGH)

    flipped = jnp.swapaxes(jnp.flip(w_second, (0, 1, 2)), 3, 4)
    second_x = columns(unfold(second_h), layer_count, 3)
    active_grad = jnp.dot(second_x, banded(flipped).reshape(-1, width), preferred_element_type=F32)
    active_grad = active_grad.reshape(showers, layer_count, GR, GP, channels)
    sigmoid_z = jax.nn.sigmoid(first)
    first_grad = (active_grad * sigmoid_z * (1.0 + first * (1.0 - sigmoid_z))).astype(BF16)
    product = lax.dot_general(
        first_grad.reshape(rows, width), grid_x, (((0,), (0,)), ((), ())),
        preferred_element_type=F32,
    ).reshape(BLK, channels, 3, 3, BLK + 2, channels)
    grad_first = jnp.einsum("mqp,poijqc->ijmco", selector(), product, precision=HIGH)

    size = grad_first.size
    flat = jnp.concatenate([grad_first.reshape(-1), grad_second.reshape(-1), grad_out])
    flat = tree_sum(flat, ("slab", "lay"))
    grad_first = flat[:size].reshape(grad_first.shape)
    grad_second = flat[size : 2 * size].reshape(grad_first.shape)
    grad_out = flat[2 * size :]
    return (predicted, grad_first, grad_second, grad_out)


def solution(mesh):
    in_specs = (
        P("slab", "lay", None, None, None),
        P("slab", "lay", None, None),
        P("lay", None, None, None),
        P("lay", None),
        P("lay"),
        P(),
        P(),
        P(),
    )
    out_specs = (P("slab", "lay", None, None), P(), P(), P())
    return jax.shard_map(
        per_device, mesh=mesh, in_specs=in_specs, out_specs=out_specs, check_vma=False
    )
```

```python
import jax
import jax.numpy as jnp
from jax import lax
from jax.sharding import PartitionSpec as P

GR = 64
GP = 64
BLK = 8

F32 = jnp.float32
BF16 = jnp.bfloat16
HIGH = lax.Precision.HIGHEST


def layer_halo(x):
    count = lax.axis_size("lay")
    if count == 1:
        zeros = jnp.zeros_like(x[:, :1])
        return jnp.concatenate([zeros, x, zeros], axis=1)
    below = lax.ppermute(x[:, -1:], "lay", [(i, i + 1) for i in range(count - 1)])
    above = lax.ppermute(x[:, :1], "lay", [(i + 1, i) for i in range(count - 1)])
    return jnp.concatenate([below, x, above], axis=1)


def unfold(x):
    s, d, r, p, c = x.shape
    main = x.reshape(s, d, r, p // BLK, BLK * c)
    left = jnp.roll(main[..., (BLK - 1) * c :], 1, axis=3)
    right = jnp.roll(main[..., :c], -1, axis=3)
    full = jnp.concatenate([left, main, right], axis=-1)
    return jnp.pad(full, ((0, 0), (0, 0), (1, 1), (0, 0), (0, 0)))


def selector():
    shape = (3, BLK + 2, BLK)
    rows_idx = lax.broadcasted_iota(jnp.int32, shape, 1)
    cols_idx = lax.broadcasted_iota(jnp.int32, shape, 2)
    tap_idx = lax.broadcasted_iota(jnp.int32, shape, 0)
    return (rows_idx == cols_idx + tap_idx).astype(F32)


def banded(weight):
    c, o = weight.shape[3], weight.shape[4]
    stack = weight.reshape(3, 3, 3 * c, o)
    blocks = [jnp.pad(stack, ((0, 0), (0, 0), (t * c, (BLK - 1 - t) * c), (0, 0))) for t in range(BLK)]
    return jnp.concatenate(blocks, axis=-1)


def conv_taps(xu, matrices, layers, layer_taps):
    radial = xu.shape[2] - 2
    total = None
    for i in range(layer_taps):
        for j in range(3):
            window = xu[:, i : i + layers, j : j + radial]
            term = jnp.dot(window.reshape(-1, window.shape[-1]), matrices[i, j],
                           preferred_element_type=F32)
            total = term if total is None else total + term
    return total


def band_take(product, c, o):
    taps = []
    for m in range(3):
        total = None
        for t in range(BLK):
            piece = product[:, t, :, :, t + m, :]
            total = piece if total is None else total + piece
        taps.append(jnp.transpose(total, (0, 2, 3, 1)))
    return jnp.stack(taps, axis=2)


def columns(xu, layers, layer_taps):
    radial = xu.shape[2] - 2
    pieces = [xu[:, i : i + layers, j : j + radial] for i in range(layer_taps) for j in range(3)]
    x = jnp.concatenate(pieces, axis=-1)
    return x.reshape(-1, x.shape[-1])


def tree_sum(x, axes):
    for axis in axes:
        size = lax.axis_size(axis)
        if size & (size - 1):
            x = lax.psum(x, axis)
            continue
        step = 1
        while step < size:
            x = x + lax.ppermute(x, axis, [(i, i ^ step) for i in range(size)])
            step *= 2
    return x


def per_device(cells, noise, geometry, tile_block, tile_count, w_first, w_second, w_out):
    showers, layer_count, tile_total, channels, cell_width = cells.shape
    block_total = GR * GP // 128
    slab_count = lax.axis_size("slab")
    lay_count = lax.axis_size("lay")
    nq = GP // BLK
    live_mask = lax.broadcasted_iota(jnp.int32, (layer_count, tile_total), 1) < tile_count[:, None]
    block_ids = lax.broadcasted_iota(jnp.int32, (layer_count, tile_total, block_total), 2)
    onehot = (live_mask[:, :, None] & (tile_block[:, :, None] == block_ids)).astype(F32)
    out_weight = w_out.astype(F32)

    mapped = jnp.einsum("bltcn,ltnp->bltcp", cells, geometry, preferred_element_type=F32)
    grid_sum = jnp.einsum("bltcp,ltk->blkpc", mapped, onehot, precision=HIGH)
    grid = grid_sum.astype(BF16).reshape(showers, layer_count, GR, GP, channels)

    rows = showers * layer_count * GR * nq
    width = BLK * channels
    grid_u = unfold(layer_halo(grid))
    first = conv_taps(grid_u, banded(w_first), layer_count, 3)
    first = first.reshape(showers, layer_count, GR, GP, channels)
    active = jax.nn.silu(first).astype(BF16)

    active_u = unfold(active)
    second_band = jnp.concatenate([banded(w_second)[i] for i in range(3)], axis=-1)
    parts = conv_taps(active_u, second_band[None], layer_count, 1)
    lane = lax.broadcasted_iota(jnp.int32, (3 * width, 3 * BLK), 0)
    slot = lax.broadcasted_iota(jnp.int32, (3 * width, 3 * BLK), 1)
    project = jnp.where(lane // channels == slot, jnp.tile(out_weight, 3 * BLK)[:, None], 0.0)
    projected = jnp.dot(parts, project, precision=HIGH)
    projected = projected.reshape(showers, layer_count, GR, nq, 3, BLK)
    projected = jnp.transpose(projected, (4, 0, 1, 2, 3, 5)).reshape(3, showers, layer_count, GR, GP)
    lower = layer_halo(projected[0])[:, :layer_count]
    upper = layer_halo(projected[2])[:, 2:]
    grid_f = grid.astype(F32)
    own = jnp.einsum("blrpc,c->blrp", grid_f, out_weight, precision=HIGH)
    pred_grid = (own + projected[1] + lower + upper).astype(BF16)

    block_grid = pred_grid.reshape(showers, layer_count, block_total, 128)
    picked = jnp.einsum(
        "blkp,ltk->bltp", block_grid, onehot.astype(BF16), preferred_element_type=F32
    ).astype(BF16)
    predicted = jnp.einsum(
        "bltp,ltnp->bltn", picked, geometry, preferred_element_type=F32
    ).astype(BF16)
    loss_scale = 32.0 / (showers * slab_count * layer_count * lay_count * GR * GP)
    live_f = live_mask.astype(F32)[None, :, :, None]
    cell_grad = (
        (predicted.astype(F32) - noise.astype(F32)) * live_f * loss_scale
    ).astype(BF16)
    back_map = jnp.einsum("bltn,ltnp->bltp", cell_grad, geometry, preferred_element_type=F32)
    grid_grad = jnp.einsum("bltp,ltk->blkp", back_map, onehot, precision=HIGH)
    grid_grad = grid_grad.astype(BF16).reshape(showers, layer_count, GR, GP)

    grad_h = layer_halo(grid_grad).astype(F32)
    taps_grad = jnp.stack(
        [grad_h[:, 2 - i : 2 - i + layer_count].reshape(showers, layer_count, GR, nq, BLK)
         for i in range(3)],
        axis=4,
    ).reshape(rows, 3 * BLK)
    grad_out = jnp.einsum("blrpc,blrp->c", grid_f, grad_h[:, 1 : 1 + layer_count], precision=HIGH)
    weighted = parts.reshape(rows, 3 * BLK, channels) * taps_grad[:, :, None]
    grad_out = grad_out + jnp.sum(weighted, axis=(0, 1))

    second_h = (grad_h[..., None] * out_weight).astype(BF16)
    taps_second = jnp.concatenate(
        [second_h[:, 2 - i : 2 - i + layer_count].reshape(rows, width) for i in range(3)], axis=-1
    )
    product = lax.dot_general(
        taps_second, columns(active_u, layer_count, 1), (((0,), (0,)), ((), ())),
        preferred_element_type=F32,
    ).reshape(3, BLK, channels, 3, BLK + 2, channels)
    grad_second = band_take(product, channels, channels)

    flipped = jnp.swapaxes(jnp.flip(w_second, (0, 1, 2)), 3, 4)
    active_grad = conv_taps(unfold(second_h), banded(flipped), layer_count, 3)
    active_grad = active_grad.reshape(showers, layer_count, GR, GP, channels)
    sigmoid_z = jax.nn.sigmoid(first)
    first_grad = (active_grad * sigmoid_z * (1.0 + first * (1.0 - sigmoid_z))).astype(BF16)
    product = lax.dot_general(
        first_grad.reshape(rows, width), columns(grid_u, layer_count, 3), (((0,), (0,)), ((), ())),
        preferred_element_type=F32,
    ).reshape(1, BLK, channels, 9, BLK + 2, channels)
    grad_first = band_take(product, channels, channels).reshape(3, 3, 3, channels, channels)

    size = grad_first.size
    flat = jnp.concatenate([grad_first.reshape(-1), grad_second.reshape(-1), grad_out])
    flat = tree_sum(flat, ("slab", "lay"))
    grad_first = flat[:size].reshape(grad_first.shape)
    grad_second = flat[size : 2 * size].reshape(grad_first.shape)
    grad_out = flat[2 * size :]
    return (predicted, grad_first, grad_second, grad_out)


def solution(mesh):
    in_specs = (
        P("slab", "lay", None, None, None),
        P("slab", "lay", None, None),
        P("lay", None, None, None),
        P("lay", None),
        P("lay"),
        P(),
        P(),
        P(),
    )
    out_specs = (P("slab", "lay", None, None), P(), P(), P())
    return jax.shard_map(
        per_device, mesh=mesh, in_specs=in_specs, out_specs=out_specs, check_vma=False
    )
```

```python
import jax
import jax.numpy as jnp
from jax import lax
from jax.experimental import pallas as pl
from jax.sharding import PartitionSpec as P

GR = 64
GP = 64
BLK = 8

F32 = jnp.float32
BF16 = jnp.bfloat16
HIGH = lax.Precision.HIGHEST


def layer_halo(x):
    count = lax.axis_size("lay")
    if count == 1:
        zeros = jnp.zeros_like(x[:, :1])
        return jnp.concatenate([zeros, x, zeros], axis=1)
    below = lax.ppermute(x[:, -1:], "lay", [(i, i + 1) for i in range(count - 1)])
    above = lax.ppermute(x[:, :1], "lay", [(i + 1, i) for i in range(count - 1)])
    return jnp.concatenate([below, x, above], axis=1)


def unfold(x, c):
    left = jnp.roll(x[..., (BLK - 1) * c :], 1, axis=3)
    right = jnp.roll(x[..., :c], -1, axis=3)
    full = jnp.concatenate([left, x, right], axis=-1).astype(F32)
    return jnp.pad(full, ((0, 0), (0, 0), (1, 1), (0, 0), (0, 0)))


def conv_fwd(xu, mats, layers):
    s_n, _, rp, q_n, k_n = xu.shape
    t_n, n_n = mats.shape[0], mats.shape[3]
    radial = rp - 2

    def kernel(x_ref, m_ref, o_ref):
        for s in range(s_n):
            for l in range(layers):
                acc = None
                for i in range(t_n):
                    for j in range(3):
                        win = x_ref[s, l + i, j : j + radial].reshape(radial * q_n, k_n).astype(BF16)
                        term = jnp.dot(win, m_ref[i, j], preferred_element_type=F32)
                        acc = term if acc is None else acc + term
                o_ref[s, l] = acc

    return pl.pallas_call(
        kernel, out_shape=jax.ShapeDtypeStruct((s_n, layers, radial * q_n, n_n), F32)
    )(xu, mats)


def conv_wgrad(xu, grad_t, layer_taps):
    s_n, _, rp, q_n, k_n = xu.shape
    layers, n_n = grad_t.shape[1], grad_t.shape[2]
    radial = rp - 2

    def kernel(x_ref, g_ref, o_ref):
        for i in range(layer_taps):
            for j in range(3):
                acc = None
                for s in range(s_n):
                    for l in range(layers):
                        win = x_ref[s, l + i, j : j + radial].reshape(radial * q_n, k_n).astype(BF16)
                        term = jnp.dot(g_ref[s, l], win, preferred_element_type=F32)
                        acc = term if acc is None else acc + term
                o_ref[i, j] = acc

    return pl.pallas_call(
        kernel, out_shape=jax.ShapeDtypeStruct((layer_taps, 3, n_n, k_n), F32)
    )(xu, grad_t)


def selector():
    shape = (3, BLK + 2, BLK)
    rows_idx = lax.broadcasted_iota(jnp.int32, shape, 1)
    cols_idx = lax.broadcasted_iota(jnp.int32, shape, 2)
    tap_idx = lax.broadcasted_iota(jnp.int32, shape, 0)
    return (rows_idx == cols_idx + tap_idx).astype(F32)


def banded(weight):
    c, o = weight.shape[3], weight.shape[4]
    stack = weight.reshape(3, 3, 3 * c, o)
    blocks = [jnp.pad(stack, ((0, 0), (0, 0), (t * c, (BLK - 1 - t) * c), (0, 0))) for t in range(BLK)]
    return jnp.concatenate(blocks, axis=-1)


def band_take(product, c, o):
    taps = []
    for m in range(3):
        total = None
        for t in range(BLK):
            piece = product[:, t, :, :, t + m, :]
            total = piece if total is None else total + piece
        taps.append(jnp.transpose(total, (0, 2, 3, 1)))
    return jnp.stack(taps, axis=2)


def tree_sum(x, axes):
    for axis in axes:
        size = lax.axis_size(axis)
        if size & (size - 1):
            x = lax.psum(x, axis)
            continue
        step = 1
        while step < size:
            x = x + lax.ppermute(x, axis, [(i, i ^ step) for i in range(size)])
            step *= 2
    return x


def per_device(cells, noise, geometry, tile_block, tile_count, w_first, w_second, w_out):
    showers, layer_count, tile_total, channels, cell_width = cells.shape
    block_total = GR * GP // 128
    slab_count = lax.axis_size("slab")
    lay_count = lax.axis_size("lay")
    nq = GP // BLK
    live_mask = lax.broadcasted_iota(jnp.int32, (layer_count, tile_total), 1) < tile_count[:, None]
    block_ids = lax.broadcasted_iota(jnp.int32, (layer_count, tile_total, block_total), 2)
    onehot = (live_mask[:, :, None] & (tile_block[:, :, None] == block_ids)).astype(F32)
    out_weight = w_out.astype(F32)

    mapped = jnp.einsum("bltcn,ltnp->bltcp", cells, geometry, preferred_element_type=F32)
    grid_sum = jnp.einsum("bltcp,ltk->blkpc", mapped, onehot, precision=HIGH)
    rows = showers * layer_count * GR * nq
    width = BLK * channels
    grid = grid_sum.astype(BF16).reshape(showers, layer_count, GR, nq, width)

    grid_u = unfold(layer_halo(grid), channels)
    first = conv_fwd(grid_u, banded(w_first), layer_count)
    first = first.reshape(showers, layer_count, GR, nq, width)
    active = jax.nn.silu(first).astype(BF16)

    active_u = unfold(active, channels)
    second_band = jnp.concatenate([banded(w_second)[i] for i in range(3)], axis=-1)
    parts = conv_fwd(active_u, second_band[None], layer_count).reshape(rows, 3 * width)
    lane = lax.broadcasted_iota(jnp.int32, (3 * width, 3 * BLK), 0)
    slot = lax.broadcasted_iota(jnp.int32, (3 * width, 3 * BLK), 1)
    project = jnp.where(lane // channels == slot, jnp.tile(out_weight, 3 * BLK)[:, None], 0.0)
    projected = jnp.dot(parts, project, precision=HIGH)
    projected = projected.reshape(showers, layer_count, GR, nq, 3, BLK)
    projected = jnp.transpose(projected, (4, 0, 1, 2, 3, 5)).reshape(3, showers, layer_count, GR, GP)
    lower = layer_halo(projected[0])[:, :layer_count]
    upper = layer_halo(projected[2])[:, 2:]
    grid_f = grid.astype(F32).reshape(showers, layer_count, GR, nq, BLK, channels)
    own = jnp.einsum("blrqtc,c->blrqt", grid_f, out_weight, precision=HIGH)
    own = own.reshape(showers, layer_count, GR, GP)
    pred_grid = (own + projected[1] + lower + upper).astype(BF16)

    block_grid = pred_grid.reshape(showers, layer_count, block_total, 128)
    picked = jnp.einsum(
        "blkp,ltk->bltp", block_grid, onehot.astype(BF16), preferred_element_type=F32
    ).astype(BF16)
    predicted = jnp.einsum(
        "bltp,ltnp->bltn", picked, geometry, preferred_element_type=F32
    ).astype(BF16)
    loss_scale = 32.0 / (showers * slab_count * layer_count * lay_count * GR * GP)
    live_f = live_mask.astype(F32)[None, :, :, None]
    cell_grad = (
        (predicted.astype(F32) - noise.astype(F32)) * live_f * loss_scale
    ).astype(BF16)
    back_map = jnp.einsum("bltn,ltnp->bltp", cell_grad, geometry, preferred_element_type=F32)
    grid_grad = jnp.einsum("bltp,ltk->blkp", back_map, onehot, precision=HIGH)
    grid_grad = grid_grad.astype(BF16).reshape(showers, layer_count, GR, nq, BLK)

    grad_h = layer_halo(grid_grad).astype(F32)
    taps_grad = jnp.stack(
        [grad_h[:, 2 - i : 2 - i + layer_count] for i in range(3)], axis=4
    ).reshape(rows, 3 * BLK)
    grad_out = jnp.einsum("blrqtc,blrqt->c", grid_f, grad_h[:, 1 : 1 + layer_count], precision=HIGH)
    weighted = parts.reshape(rows, 3 * BLK, channels) * taps_grad[:, :, None]
    grad_out = grad_out + jnp.sum(weighted, axis=(0, 1))

    second_h = (grad_h[..., None] * out_weight).astype(BF16)
    second_h = second_h.reshape(showers, layer_count + 2, GR, nq, width)
    taps_second = jnp.concatenate(
        [second_h[:, 2 - i : 2 - i + layer_count] for i in range(3)], axis=-1
    ).reshape(showers, layer_count, GR * nq, 3 * width)
    product = conv_wgrad(active_u, jnp.swapaxes(taps_second, 2, 3), 1)
    product = product.reshape(3, 3, BLK, channels, BLK + 2, channels)
    grad_second = band_take(jnp.transpose(product, (1, 2, 3, 0, 4, 5)), channels, channels)

    flipped = jnp.swapaxes(jnp.flip(w_second, (0, 1, 2)), 3, 4)
    active_grad = conv_fwd(unfold(second_h, channels), banded(flipped), layer_count)
    active_grad = active_grad.reshape(showers, layer_count, GR, nq, width)
    sigmoid_z = jax.nn.sigmoid(first)
    first_grad = (active_grad * sigmoid_z * (1.0 + first * (1.0 - sigmoid_z))).astype(BF16)
    first_grad = first_grad.reshape(showers, layer_count, GR * nq, width)
    product = conv_wgrad(grid_u, jnp.swapaxes(first_grad, 2, 3), 3)
    product = product.reshape(9, BLK, channels, BLK + 2, channels)
    product = jnp.transpose(product, (1, 2, 0, 3, 4))[None]
    grad_first = band_take(product, channels, channels).reshape(3, 3, 3, channels, channels)

    size = grad_first.size
    flat = jnp.concatenate([grad_first.reshape(-1), grad_second.reshape(-1), grad_out])
    flat = tree_sum(flat, ("slab", "lay"))
    grad_first = flat[:size].reshape(grad_first.shape)
    grad_second = flat[size : 2 * size].reshape(grad_first.shape)
    grad_out = flat[2 * size :]
    return (predicted, grad_first, grad_second, grad_out)


def solution(mesh):
    in_specs = (
        P("slab", "lay", None, None, None),
        P("slab", "lay", None, None),
        P("lay", None, None, None),
        P("lay", None),
        P("lay"),
        P(),
        P(),
        P(),
    )
    out_specs = (P("slab", "lay", None, None), P(), P(), P())
    return jax.shard_map(
        per_device, mesh=mesh, in_specs=in_specs, out_specs=out_specs, check_vma=False
    )
```

```python
import jax
import jax.numpy as jnp
from jax import lax
from jax.experimental import pallas as pl
from jax.sharding import PartitionSpec as P

GR = 64
GP = 64
BLK = 8

F32 = jnp.float32
BF16 = jnp.bfloat16
HIGH = lax.Precision.HIGHEST


def layer_halo(x):
    count = lax.axis_size("lay")
    if count == 1:
        zeros = jnp.zeros_like(x[:, :1])
        return jnp.concatenate([zeros, x, zeros], axis=1)
    below = lax.ppermute(x[:, -1:], "lay", [(i, i + 1) for i in range(count - 1)])
    above = lax.ppermute(x[:, :1], "lay", [(i + 1, i) for i in range(count - 1)])
    return jnp.concatenate([below, x, above], axis=1)


def unfold(x, c):
    left = jnp.roll(x[..., (BLK - 1) * c :], 1, axis=3)
    right = jnp.roll(x[..., :c], -1, axis=3)
    full = jnp.concatenate([left, x, right], axis=-1).astype(F32)
    return jnp.pad(full, ((0, 0), (0, 0), (1, 1), (0, 0), (0, 0)))


def conv_fwd(xu, mats, layers):
    s_n, _, rp, q_n, k_n = xu.shape
    t_n, n_n = mats.shape[0], mats.shape[3]
    radial = rp - 2

    def kernel(x_ref, m_ref, o_ref):
        for s in range(s_n):
            for l in range(layers):
                acc = None
                for i in range(t_n):
                    for j in range(3):
                        win = x_ref[s, l + i, j : j + radial].reshape(radial * q_n, k_n).astype(BF16)
                        term = jnp.dot(win, m_ref[i, j], preferred_element_type=F32)
                        acc = term if acc is None else acc + term
                o_ref[s, l] = acc

    return pl.pallas_call(
        kernel, out_shape=jax.ShapeDtypeStruct((s_n, layers, radial * q_n, n_n), F32)
    )(xu, mats)


def conv_wgrad(xu, grad_t, layer_taps):
    s_n, _, rp, q_n, k_n = xu.shape
    layers, n_n = grad_t.shape[1], grad_t.shape[2]
    radial = rp - 2

    def kernel(x_ref, g_ref, o_ref):
        for i in range(layer_taps):
            for j in range(3):
                acc = None
                for s in range(s_n):
                    for l in range(layers):
                        win = x_ref[s, l + i, j : j + radial].reshape(radial * q_n, k_n).astype(BF16)
                        term = jnp.dot(g_ref[s, l], win, preferred_element_type=F32)
                        acc = term if acc is None else acc + term
                o_ref[i, j] = acc

    return pl.pallas_call(
        kernel, out_shape=jax.ShapeDtypeStruct((layer_taps, 3, n_n, k_n), F32)
    )(xu, grad_t)


def selector():
    shape = (3, BLK + 2, BLK)
    rows_idx = lax.broadcasted_iota(jnp.int32, shape, 1)
    cols_idx = lax.broadcasted_iota(jnp.int32, shape, 2)
    tap_idx = lax.broadcasted_iota(jnp.int32, shape, 0)
    return (rows_idx == cols_idx + tap_idx).astype(F32)


def banded(weight):
    lead, c, o = weight.shape[:-3], weight.shape[-2], weight.shape[-1]
    stack = weight.reshape(lead + (3 * c, o))
    rim = [(0, 0)] * len(lead)
    blocks = [jnp.pad(stack, rim + [(t * c, (BLK - 1 - t) * c), (0, 0)]) for t in range(BLK)]
    return jnp.concatenate(blocks, axis=-1)


def band_take(product, c, o):
    taps = []
    for m in range(3):
        total = None
        for t in range(BLK):
            piece = product[:, t, :, :, t + m, :]
            total = piece if total is None else total + piece
        taps.append(jnp.transpose(total, (0, 2, 3, 1)))
    return jnp.stack(taps, axis=2)


def tree_sum(x, axes):
    for axis in axes:
        size = lax.axis_size(axis)
        if size & (size - 1):
            x = lax.psum(x, axis)
            continue
        step = 1
        while step < size:
            x = x + lax.ppermute(x, axis, [(i, i ^ step) for i in range(size)])
            step *= 2
    return x


def per_device(cells, noise, geometry, tile_block, tile_count, w_first, w_second, w_out):
    showers, layer_count, tile_total, channels, cell_width = cells.shape
    block_total = GR * GP // 128
    slab_count = lax.axis_size("slab")
    lay_count = lax.axis_size("lay")
    nq = GP // BLK
    live_mask = lax.broadcasted_iota(jnp.int32, (layer_count, tile_total), 1) < tile_count[:, None]
    block_ids = lax.broadcasted_iota(jnp.int32, (layer_count, tile_total, block_total), 2)
    onehot = (live_mask[:, :, None] & (tile_block[:, :, None] == block_ids)).astype(F32)
    out_weight = w_out.astype(F32)

    mapped = jnp.einsum("bltcn,ltnp->bltcp", cells, geometry, preferred_element_type=F32)
    grid_sum = jnp.einsum("bltcp,ltk->blkpc", mapped, onehot, precision=HIGH)
    rows = showers * layer_count * GR * nq
    width = BLK * channels
    grid = grid_sum.astype(BF16).reshape(showers, layer_count, GR, nq, width)

    flipped = jnp.swapaxes(jnp.flip(w_second, (0, 1, 2)), 3, 4)
    bands = banded(jnp.stack([w_first, w_second, flipped], axis=2))
    grid_u = unfold(layer_halo(grid), channels)
    first = conv_fwd(grid_u, bands[:, :, 0], layer_count)
    first = first.reshape(showers, layer_count, GR, nq, width)
    active = jax.nn.silu(first).astype(BF16)

    active_u = unfold(active, channels)
    second_band = jnp.concatenate([bands[i, :, 1] for i in range(3)], axis=-1)
    parts = conv_fwd(active_u, second_band[None], layer_count).reshape(rows, 3 * width)
    lane = lax.broadcasted_iota(jnp.int32, (3 * width, 3 * BLK), 0)
    slot = lax.broadcasted_iota(jnp.int32, (3 * width, 3 * BLK), 1)
    project = jnp.where(lane // channels == slot, jnp.tile(out_weight, 3 * BLK)[:, None], 0.0)
    projected = jnp.dot(parts, project, precision=HIGH)
    projected = projected.reshape(showers, layer_count, GR, nq, 3, BLK)
    projected = jnp.transpose(projected, (4, 0, 1, 2, 3, 5)).reshape(3, showers, layer_count, GR, GP)
    lower = layer_halo(projected[0])[:, :layer_count]
    upper = layer_halo(projected[2])[:, 2:]
    grid_f = grid.astype(F32).reshape(showers, layer_count, GR, nq, BLK, channels)
    own = jnp.einsum("blrqtc,c->blrqt", grid_f, out_weight, precision=HIGH)
    own = own.reshape(showers, layer_count, GR, GP)
    pred_grid = (own + projected[1] + lower + upper).astype(BF16)

    block_grid = pred_grid.reshape(showers, layer_count, block_total, 128)
    picked = jnp.einsum(
        "blkp,ltk->bltp", block_grid, onehot.astype(BF16), preferred_element_type=F32
    ).astype(BF16)
    predicted = jnp.einsum(
        "bltp,ltnp->bltn", picked, geometry, preferred_element_type=F32
    ).astype(BF16)
    loss_scale = 32.0 / (showers * slab_count * layer_count * lay_count * GR * GP)
    live_f = live_mask.astype(F32)[None, :, :, None]
    cell_grad = (
        (predicted.astype(F32) - noise.astype(F32)) * live_f * loss_scale
    ).astype(BF16)
    back_map = jnp.einsum("bltn,ltnp->bltp", cell_grad, geometry, preferred_element_type=F32)
    grid_grad = jnp.einsum("bltp,ltk->blkp", back_map, onehot, precision=HIGH)
    grid_grad = grid_grad.astype(BF16).reshape(showers, layer_count, GR, nq, BLK)

    grad_h = layer_halo(grid_grad).astype(F32)
    taps_grad = jnp.stack(
        [grad_h[:, 2 - i : 2 - i + layer_count] for i in range(3)], axis=4
    ).reshape(rows, 3 * BLK)
    grad_out = jnp.einsum("blrqtc,blrqt->c", grid_f, grad_h[:, 1 : 1 + layer_count], precision=HIGH)
    weighted = parts.reshape(rows, 3 * BLK, channels) * taps_grad[:, :, None]
    grad_out = grad_out + jnp.sum(weighted, axis=(0, 1))

    second_h = (grad_h[..., None] * out_weight).astype(BF16)
    second_h = second_h.reshape(showers, layer_count + 2, GR, nq, width)
    taps_second = jnp.concatenate(
        [second_h[:, 2 - i : 2 - i + layer_count] for i in range(3)], axis=-1
    ).reshape(showers, layer_count, GR * nq, 3 * width)
    product = conv_wgrad(active_u, jnp.swapaxes(taps_second, 2, 3), 1)
    product = product.reshape(3, 3, BLK, channels, BLK + 2, channels)
    grad_second = band_take(jnp.transpose(product, (1, 2, 3, 0, 4, 5)), channels, channels)

    early = tree_sum(jnp.concatenate([grad_second.reshape(-1), grad_out]), ("slab", "lay"))
    active_grad = conv_fwd(unfold(second_h, channels), bands[:, :, 2], layer_count)
    active_grad = active_grad.reshape(showers, layer_count, GR, nq, width)
    sigmoid_z = jax.nn.sigmoid(first)
    first_grad = (active_grad * sigmoid_z * (1.0 + first * (1.0 - sigmoid_z))).astype(BF16)
    first_grad = first_grad.reshape(showers, layer_count, GR * nq, width)
    product = conv_wgrad(grid_u, jnp.swapaxes(first_grad, 2, 3), 3)
    product = product.reshape(9, BLK, channels, BLK + 2, channels)
    product = jnp.transpose(product, (1, 2, 0, 3, 4))[None]
    grad_first = band_take(product, channels, channels).reshape(3, 3, 3, channels, channels)

    size = grad_first.size
    grad_first = tree_sum(grad_first.reshape(-1), ("slab", "lay")).reshape(grad_first.shape)
    grad_second = early[:size].reshape(grad_first.shape)
    grad_out = early[size:]
    return (predicted, grad_first, grad_second, grad_out)


def solution(mesh):
    in_specs = (
        P("slab", "lay", None, None, None),
        P("slab", "lay", None, None),
        P("lay", None, None, None),
        P("lay", None),
        P("lay"),
        P(),
        P(),
        P(),
    )
    out_specs = (P("slab", "lay", None, None), P(), P(), P())
    return jax.shard_map(
        per_device, mesh=mesh, in_specs=in_specs, out_specs=out_specs, check_vma=False
    )
```

```python
import jax
import jax.numpy as jnp
from jax import lax
from jax.experimental import pallas as pl
from jax.sharding import PartitionSpec as P

GR = 64
GP = 64
BLK = 8

F32 = jnp.float32
BF16 = jnp.bfloat16
HIGH = lax.Precision.HIGHEST


def layer_halo(x):
    count = lax.axis_size("lay")
    if count == 1:
        zeros = jnp.zeros_like(x[:, :1])
        return jnp.concatenate([zeros, x, zeros], axis=1)
    below = lax.ppermute(x[:, -1:], "lay", [(i, i + 1) for i in range(count - 1)])
    above = lax.ppermute(x[:, :1], "lay", [(i + 1, i) for i in range(count - 1)])
    return jnp.concatenate([below, x, above], axis=1)


def unfold(x, c):
    left = jnp.roll(x[..., (BLK - 1) * c :], 1, axis=3)
    right = jnp.roll(x[..., :c], -1, axis=3)
    full = jnp.concatenate([left, x, right], axis=-1).astype(F32)
    return jnp.pad(full, ((0, 0), (0, 0), (1, 1), (0, 0), (0, 0)))


def conv_fwd(xu, mats, layers):
    s_n, _, rp, q_n, k_n = xu.shape
    t_n, n_n = mats.shape[0], mats.shape[3]
    radial = rp - 2

    def kernel(x_ref, m_ref, o_ref):
        for s in range(s_n):
            for l in range(layers):
                acc = None
                for i in range(t_n):
                    for j in range(3):
                        win = x_ref[s, l + i, j : j + radial].reshape(radial * q_n, k_n).astype(BF16)
                        term = jnp.dot(win, m_ref[i, j], preferred_element_type=F32)
                        acc = term if acc is None else acc + term
                o_ref[s, l] = acc

    return pl.pallas_call(
        kernel, out_shape=jax.ShapeDtypeStruct((s_n, layers, radial * q_n, n_n), F32)
    )(xu, mats)


def conv_wgrad(xu, grad_t, layer_taps, c):
    s_n, _, rp, q_n, k_n = xu.shape
    layers, n_n = grad_t.shape[1], grad_t.shape[2]
    radial = rp - 2
    groups = n_n // (BLK * c)

    def kernel(x_ref, g_ref, o_ref):
        for i in range(layer_taps):
            for j in range(3):
                acc = None
                for s in range(s_n):
                    for l in range(layers):
                        win = x_ref[s, l + i, j : j + radial].reshape(radial * q_n, k_n).astype(BF16)
                        term = jnp.dot(g_ref[s, l], win, preferred_element_type=F32)
                        acc = term if acc is None else acc + term
                for g in range(groups):
                    for m in range(3):
                        band = None
                        for t in range(BLK):
                            row = (g * BLK + t) * c
                            piece = acc[row : row + c, (t + m) * c : (t + m + 1) * c]
                            band = piece if band is None else band + piece
                        o_ref[i, j, g, m] = band

    return pl.pallas_call(
        kernel, out_shape=jax.ShapeDtypeStruct((layer_taps, 3, groups, 3, c, c), F32)
    )(xu, grad_t)


def selector():
    shape = (3, BLK + 2, BLK)
    rows_idx = lax.broadcasted_iota(jnp.int32, shape, 1)
    cols_idx = lax.broadcasted_iota(jnp.int32, shape, 2)
    tap_idx = lax.broadcasted_iota(jnp.int32, shape, 0)
    return (rows_idx == cols_idx + tap_idx).astype(F32)


def banded(weight):
    lead, c, o = weight.shape[:-3], weight.shape[-2], weight.shape[-1]
    stack = weight.reshape(lead + (3 * c, o))
    rim = [(0, 0)] * len(lead)
    blocks = [jnp.pad(stack, rim + [(t * c, (BLK - 1 - t) * c), (0, 0)]) for t in range(BLK)]
    return jnp.concatenate(blocks, axis=-1)


def tree_sum(x, axes):
    for axis in axes:
        size = lax.axis_size(axis)
        if size & (size - 1):
            x = lax.psum(x, axis)
            continue
        step = 1
        while step < size:
            x = x + lax.ppermute(x, axis, [(i, i ^ step) for i in range(size)])
            step *= 2
    return x


def per_device(cells, noise, geometry, tile_block, tile_count, w_first, w_second, w_out):
    showers, layer_count, tile_total, channels, cell_width = cells.shape
    block_total = GR * GP // 128
    slab_count = lax.axis_size("slab")
    lay_count = lax.axis_size("lay")
    nq = GP // BLK
    live_mask = lax.broadcasted_iota(jnp.int32, (layer_count, tile_total), 1) < tile_count[:, None]
    block_ids = lax.broadcasted_iota(jnp.int32, (layer_count, tile_total, block_total), 2)
    onehot = (live_mask[:, :, None] & (tile_block[:, :, None] == block_ids)).astype(F32)
    out_weight = w_out.astype(F32)

    mapped = jnp.einsum("bltcn,ltnp->bltcp", cells, geometry, preferred_element_type=F32)
    grid_sum = jnp.einsum("bltcp,ltk->blkpc", mapped, onehot, precision=HIGH)
    rows = showers * layer_count * GR * nq
    width = BLK * channels
    grid = grid_sum.astype(BF16).reshape(showers, layer_count, GR, nq, width)

    flipped = jnp.swapaxes(jnp.flip(w_second, (0, 1, 2)), 3, 4)
    bands = banded(jnp.stack([w_first, w_second, flipped], axis=2))
    grid_u = unfold(layer_halo(grid), channels)
    first = conv_fwd(grid_u, bands[:, :, 0], layer_count)
    first = first.reshape(showers, layer_count, GR, nq, width)
    active = jax.nn.silu(first).astype(BF16)

    active_u = unfold(active, channels)
    second_band = jnp.concatenate([bands[i, :, 1] for i in range(3)], axis=-1)
    parts = conv_fwd(active_u, second_band[None], layer_count).reshape(rows, 3 * width)
    lane = lax.broadcasted_iota(jnp.int32, (3 * width, 3 * BLK), 0)
    slot = lax.broadcasted_iota(jnp.int32, (3 * width, 3 * BLK), 1)
    project = jnp.where(lane // channels == slot, jnp.tile(out_weight, 3 * BLK)[:, None], 0.0)
    projected = jnp.dot(parts, project, precision=HIGH)
    projected = projected.reshape(showers, layer_count, GR, nq, 3, BLK)
    projected = jnp.transpose(projected, (4, 0, 1, 2, 3, 5)).reshape(3, showers, layer_count, GR, GP)
    lower = layer_halo(projected[0])[:, :layer_count]
    upper = layer_halo(projected[2])[:, 2:]
    grid_f = grid.astype(F32).reshape(showers, layer_count, GR, nq, BLK, channels)
    own = jnp.einsum("blrqtc,c->blrqt", grid_f, out_weight, precision=HIGH)
    own = own.reshape(showers, layer_count, GR, GP)
    pred_grid = (own + projected[1] + lower + upper).astype(BF16)

    block_grid = pred_grid.reshape(showers, layer_count, block_total, 128)
    picked = jnp.einsum(
        "blkp,ltk->bltp", block_grid, onehot.astype(BF16), preferred_element_type=F32
    ).astype(BF16)
    predicted = jnp.einsum(
        "bltp,ltnp->bltn", picked, geometry, preferred_element_type=F32
    ).astype(BF16)
    loss_scale = 32.0 / (showers * slab_count * layer_count * lay_count * GR * GP)
    live_f = live_mask.astype(F32)[None, :, :, None]
    cell_grad = (
        (predicted.astype(F32) - noise.astype(F32)) * live_f * loss_scale
    ).astype(BF16)
    back_map = jnp.einsum("bltn,ltnp->bltp", cell_grad, geometry, preferred_element_type=F32)
    grid_grad = jnp.einsum("bltp,ltk->blkp", back_map, onehot, precision=HIGH)
    grid_grad = grid_grad.astype(BF16).reshape(showers, layer_count, GR, nq, BLK)

    grad_h = layer_halo(grid_grad).astype(F32)
    taps_grad = jnp.stack(
        [grad_h[:, 2 - i : 2 - i + layer_count] for i in range(3)], axis=4
    ).reshape(rows, 3 * BLK)
    grad_out = jnp.einsum("blrqtc,blrqt->c", grid_f, grad_h[:, 1 : 1 + layer_count], precision=HIGH)
    weighted = parts.reshape(rows, 3 * BLK, channels) * taps_grad[:, :, None]
    grad_out = grad_out + jnp.sum(weighted, axis=(0, 1))

    second_h = (grad_h[..., None] * out_weight).astype(BF16)
    second_h = second_h.reshape(showers, layer_count + 2, GR, nq, width)
    taps_second = jnp.concatenate(
        [second_h[:, 2 - i : 2 - i + layer_count] for i in range(3)], axis=-1
    ).reshape(showers, layer_count, GR * nq, 3 * width)
    product = conv_wgrad(active_u, jnp.swapaxes(taps_second, 2, 3), 1, channels)
    grad_second = jnp.transpose(product[0], (1, 0, 2, 4, 3))

    early = tree_sum(jnp.concatenate([grad_second.reshape(-1), grad_out]), ("slab", "lay"))
    active_grad = conv_fwd(unfold(second_h, channels), bands[:, :, 2], layer_count)
    active_grad = active_grad.reshape(showers, layer_count, GR, nq, width)
    sigmoid_z = jax.nn.sigmoid(first)
    first_grad = (active_grad * sigmoid_z * (1.0 + first * (1.0 - sigmoid_z))).astype(BF16)
    first_grad = first_grad.reshape(showers, layer_count, GR * nq, width)
    product = conv_wgrad(grid_u, jnp.swapaxes(first_grad, 2, 3), 3, channels)
    grad_first = jnp.transpose(product[:, :, 0], (0, 1, 2, 4, 3))

    size = grad_first.size
    grad_first = tree_sum(grad_first.reshape(-1), ("slab", "lay")).reshape(grad_first.shape)
    grad_second = early[:size].reshape(grad_first.shape)
    grad_out = early[size:]
    return (predicted, grad_first, grad_second, grad_out)


def solution(mesh):
    in_specs = (
        P("slab", "lay", None, None, None),
        P("slab", "lay", None, None),
        P("lay", None, None, None),
        P("lay", None),
        P("lay"),
        P(),
        P(),
        P(),
    )
    out_specs = (P("slab", "lay", None, None), P(), P(), P())
    return jax.shard_map(
        per_device, mesh=mesh, in_specs=in_specs, out_specs=out_specs, check_vma=False
    )
```

```python
import jax
import jax.numpy as jnp
from jax import lax
from jax.experimental import pallas as pl
from jax.sharding import PartitionSpec as P

GR = 64
GP = 64
BLK = 8

F32 = jnp.float32
BF16 = jnp.bfloat16
HIGH = lax.Precision.HIGHEST


def layer_halo(x):
    count = lax.axis_size("lay")
    if count == 1:
        zeros = jnp.zeros_like(x[:, :1])
        return jnp.concatenate([zeros, x, zeros], axis=1)
    below = lax.ppermute(x[:, -1:], "lay", [(i, i + 1) for i in range(count - 1)])
    above = lax.ppermute(x[:, :1], "lay", [(i + 1, i) for i in range(count - 1)])
    return jnp.concatenate([below, x, above], axis=1)


def unfold(x, c):
    left = jnp.roll(x[..., (BLK - 1) * c :], 1, axis=3)
    right = jnp.roll(x[..., :c], -1, axis=3)
    full = jnp.concatenate([left, x, right], axis=-1).astype(F32)
    return jnp.pad(full, ((0, 0), (0, 0), (1, 1), (0, 0), (0, 0)))


def conv_fwd(xu, mats, layers):
    s_n, _, rp, q_n, k_n = xu.shape
    t_n, n_n = mats.shape[0], mats.shape[3]
    radial = rp - 2

    def kernel(x_ref, m_ref, o_ref):
        for s in range(s_n):
            for l in range(layers):
                acc = None
                for i in range(t_n):
                    for j in range(3):
                        win = x_ref[s, l + i, j : j + radial].reshape(radial * q_n, k_n).astype(BF16)
                        term = jnp.dot(win, m_ref[i, j], preferred_element_type=F32)
                        acc = term if acc is None else acc + term
                o_ref[s, l] = acc

    return pl.pallas_call(
        kernel, out_shape=jax.ShapeDtypeStruct((s_n, layers, radial * q_n, n_n), F32)
    )(xu, mats)


def conv_wgrad(xu, grad_t, layer_taps, c):
    s_n, _, rp, q_n, k_n = xu.shape
    layers, n_n = grad_t.shape[1], grad_t.shape[2]
    radial = rp - 2
    groups = n_n // (BLK * c)

    def kernel(x_ref, g_ref, o_ref):
        for i in range(layer_taps):
            for j in range(3):
                acc = None
                for s in range(s_n):
                    for l in range(layers):
                        win = x_ref[s, l + i, j : j + radial].reshape(radial * q_n, k_n).astype(BF16)
                        term = jnp.dot(g_ref[s, l], win, preferred_element_type=F32)
                        acc = term if acc is None else acc + term
                for g in range(groups):
                    for m in range(3):
                        band = None
                        for t in range(BLK):
                            row = (g * BLK + t) * c
                            piece = acc[row : row + c, (t + m) * c : (t + m + 1) * c]
                            band = piece if band is None else band + piece
                        o_ref[i, j, g, m] = band

    return pl.pallas_call(
        kernel, out_shape=jax.ShapeDtypeStruct((layer_taps, 3, groups, 3, c, c), F32)
    )(xu, grad_t)


def selector():
    shape = (3, BLK + 2, BLK)
    rows_idx = lax.broadcasted_iota(jnp.int32, shape, 1)
    cols_idx = lax.broadcasted_iota(jnp.int32, shape, 2)
    tap_idx = lax.broadcasted_iota(jnp.int32, shape, 0)
    return (rows_idx == cols_idx + tap_idx).astype(F32)


def banded(weights):
    n_w, _, _, _, c, o = weights.shape
    rows, cols = (BLK + 2) * c, BLK * o

    def kernel(w_ref, o_ref):
        spread = (lax.broadcasted_iota(jnp.int32, (o, cols), 1) % o
                  == lax.broadcasted_iota(jnp.int32, (o, cols), 0)).astype(F32)
        diag = (lax.broadcasted_iota(jnp.int32, (rows, cols), 0) // c
                - lax.broadcasted_iota(jnp.int32, (rows, cols), 1) // o)
        for w in range(n_w):
            for i in range(3):
                for j in range(3):
                    acc = jnp.zeros((rows, cols), F32)
                    for m in range(3):
                        line = jnp.dot(w_ref[w, i, j, m].astype(F32), spread, precision=HIGH,
                                       preferred_element_type=F32)
                        tiled = jnp.broadcast_to(line[None], (BLK + 2, c, cols)).reshape(rows, cols)
                        acc = jnp.where(diag == m, tiled, acc)
                    o_ref[i, j, w] = acc.astype(BF16)

    return pl.pallas_call(
        kernel, out_shape=jax.ShapeDtypeStruct((3, 3, n_w, rows, cols), BF16)
    )(weights)


def tree_sum(x, axes):
    for axis in axes:
        size = lax.axis_size(axis)
        if size & (size - 1):
            x = lax.psum(x, axis)
            continue
        step = 1
        while step < size:
            x = x + lax.ppermute(x, axis, [(i, i ^ step) for i in range(size)])
            step *= 2
    return x


def per_device(cells, noise, geometry, tile_block, tile_count, w_first, w_second, w_out):
    showers, layer_count, tile_total, channels, cell_width = cells.shape
    block_total = GR * GP // 128
    slab_count = lax.axis_size("slab")
    lay_count = lax.axis_size("lay")
    nq = GP // BLK
    live_mask = lax.broadcasted_iota(jnp.int32, (layer_count, tile_total), 1) < tile_count[:, None]
    block_ids = lax.broadcasted_iota(jnp.int32, (layer_count, tile_total, block_total), 2)
    onehot = (live_mask[:, :, None] & (tile_block[:, :, None] == block_ids)).astype(F32)
    out_weight = w_out.astype(F32)

    mapped = jnp.einsum("bltcn,ltnp->bltcp", cells, geometry, preferred_element_type=F32)
    grid_sum = jnp.einsum("bltcp,ltk->blkpc", mapped, onehot, precision=HIGH)
    rows = showers * layer_count * GR * nq
    width = BLK * channels
    grid = grid_sum.astype(BF16).reshape(showers, layer_count, GR, nq, width)

    flipped = jnp.swapaxes(jnp.flip(w_second, (0, 1, 2)), 3, 4)
    bands = banded(jnp.stack([w_first, w_second, flipped]))
    grid_u = unfold(layer_halo(grid), channels)
    first = conv_fwd(grid_u, bands[:, :, 0], layer_count)
    first = first.reshape(showers, layer_count, GR, nq, width)
    active = jax.nn.silu(first).astype(BF16)

    active_u = unfold(active, channels)
    second_band = jnp.concatenate([bands[i, :, 1] for i in range(3)], axis=-1)
    parts = conv_fwd(active_u, second_band[None], layer_count).reshape(rows, 3 * width)
    lane = lax.broadcasted_iota(jnp.int32, (3 * width, 3 * BLK), 0)
    slot = lax.broadcasted_iota(jnp.int32, (3 * width, 3 * BLK), 1)
    project = jnp.where(lane // channels == slot, jnp.tile(out_weight, 3 * BLK)[:, None], 0.0)
    projected = jnp.dot(parts, project, precision=HIGH)
    projected = projected.reshape(showers, layer_count, GR, nq, 3, BLK)
    projected = jnp.transpose(projected, (4, 0, 1, 2, 3, 5)).reshape(3, showers, layer_count, GR, GP)
    lower = layer_halo(projected[0])[:, :layer_count]
    upper = layer_halo(projected[2])[:, 2:]
    grid_f = grid.astype(F32).reshape(showers, layer_count, GR, nq, BLK, channels)
    own = jnp.einsum("blrqtc,c->blrqt", grid_f, out_weight, precision=HIGH)
    own = own.reshape(showers, layer_count, GR, GP)
    pred_grid = (own + projected[1] + lower + upper).astype(BF16)

    block_grid = pred_grid.reshape(showers, layer_count, block_total, 128)
    picked = jnp.einsum(
        "blkp,ltk->bltp", block_grid, onehot.astype(BF16), preferred_element_type=F32
    ).astype(BF16)
    predicted = jnp.einsum(
        "bltp,ltnp->bltn", picked, geometry, preferred_element_type=F32
    ).astype(BF16)
    loss_scale = 32.0 / (showers * slab_count * layer_count * lay_count * GR * GP)
    live_f = live_mask.astype(F32)[None, :, :, None]
    cell_grad = (
        (predicted.astype(F32) - noise.astype(F32)) * live_f * loss_scale
    ).astype(BF16)
    back_map = jnp.einsum("bltn,ltnp->bltp", cell_grad, geometry, preferred_element_type=F32)
    grid_grad = jnp.einsum("bltp,ltk->blkp", back_map, onehot, precision=HIGH)
    grid_grad = grid_grad.astype(BF16).reshape(showers, layer_count, GR, nq, BLK)

    grad_h = layer_halo(grid_grad).astype(F32)
    taps_grad = jnp.stack(
        [grad_h[:, 2 - i : 2 - i + layer_count] for i in range(3)], axis=4
    ).reshape(rows, 3 * BLK)
    grad_out = jnp.einsum("blrqtc,blrqt->c", grid_f, grad_h[:, 1 : 1 + layer_count], precision=HIGH)
    weighted = parts.reshape(rows, 3 * BLK, channels) * taps_grad[:, :, None]
    grad_out = grad_out + jnp.sum(weighted, axis=(0, 1))

    second_h = (grad_h[..., None] * out_weight).astype(BF16)
    second_h = second_h.reshape(showers, layer_count + 2, GR, nq, width)
    taps_second = jnp.concatenate(
        [second_h[:, 2 - i : 2 - i + layer_count] for i in range(3)], axis=-1
    ).reshape(showers, layer_count, GR * nq, 3 * width)
    product = conv_wgrad(active_u, jnp.swapaxes(taps_second, 2, 3), 1, channels)
    grad_second = jnp.transpose(product[0], (1, 0, 2, 4, 3))

    early = tree_sum(jnp.concatenate([grad_second.reshape(-1), grad_out]), ("slab", "lay"))
    active_grad = conv_fwd(unfold(second_h, channels), bands[:, :, 2], layer_count)
    active_grad = active_grad.reshape(showers, layer_count, GR, nq, width)
    sigmoid_z = jax.nn.sigmoid(first)
    first_grad = (active_grad * sigmoid_z * (1.0 + first * (1.0 - sigmoid_z))).astype(BF16)
    first_grad = first_grad.reshape(showers, layer_count, GR * nq, width)
    product = conv_wgrad(grid_u, jnp.swapaxes(first_grad, 2, 3), 3, channels)
    grad_first = jnp.transpose(product[:, :, 0], (0, 1, 2, 4, 3))

    size = grad_first.size
    grad_first = tree_sum(grad_first.reshape(-1), ("slab", "lay")).reshape(grad_first.shape)
    grad_second = early[:size].reshape(grad_first.shape)
    grad_out = early[size:]
    return (predicted, grad_first, grad_second, grad_out)


def solution(mesh):
    in_specs = (
        P("slab", "lay", None, None, None),
        P("slab", "lay", None, None),
        P("lay", None, None, None),
        P("lay", None),
        P("lay"),
        P(),
        P(),
        P(),
    )
    out_specs = (P("slab", "lay", None, None), P(), P(), P())
    return jax.shard_map(
        per_device, mesh=mesh, in_specs=in_specs, out_specs=out_specs, check_vma=False
    )
```

```python
import jax
import jax.numpy as jnp
from jax import lax
from jax.experimental import pallas as pl
from jax.sharding import PartitionSpec as P


GR = 64
GP = 64
BLK = 8

F32 = jnp.float32
BF16 = jnp.bfloat16
HIGH = lax.Precision.HIGHEST


def layer_halo(x):
    count = lax.axis_size("lay")
    if count == 1:
        zeros = jnp.zeros_like(x[:, :1])
        return jnp.concatenate([zeros, x, zeros], axis=1)
    below = lax.ppermute(x[:, -1:], "lay", [(i, i + 1) for i in range(count - 1)])
    above = lax.ppermute(x[:, :1], "lay", [(i + 1, i) for i in range(count - 1)])
    return jnp.concatenate([below, x, above], axis=1)


def unfold(x, c):
    left = jnp.roll(x[..., (BLK - 1) * c :], 1, axis=3)
    right = jnp.roll(x[..., :c], -1, axis=3)
    full = jnp.concatenate([left, x, right], axis=-1).astype(F32)
    return jnp.pad(full, ((0, 0), (0, 0), (1, 1), (0, 0), (0, 0)))


def conv_fwd(xu, mats, layers):
    s_n, _, rp, q_n, k_n = xu.shape
    t_n, n_n = mats.shape[0], mats.shape[3]
    radial = rp - 2

    def kernel(x_ref, m_ref, o_ref):
        for s in range(s_n):
            for l in range(layers):
                acc = None
                for i in range(t_n):
                    for j in range(3):
                        win = x_ref[s, l + i, j : j + radial].reshape(radial * q_n, k_n).astype(BF16)
                        term = jnp.dot(win, m_ref[i, j], preferred_element_type=F32)
                        acc = term if acc is None else acc + term
                o_ref[s, l] = acc

    return pl.pallas_call(
        kernel, out_shape=jax.ShapeDtypeStruct((s_n, layers, radial * q_n, n_n), F32)
    )(xu, mats)


def conv_wgrad(xu, grad_t, layer_taps, c):
    s_n, _, rp, q_n, k_n = xu.shape
    layers, n_n = grad_t.shape[1], grad_t.shape[2]
    radial = rp - 2
    groups = n_n // (BLK * c)

    def kernel(x_ref, g_ref, o_ref):
        for i in range(layer_taps):
            for j in range(3):
                acc = None
                for s in range(s_n):
                    for l in range(layers):
                        win = x_ref[s, l + i, j : j + radial].reshape(radial * q_n, k_n).astype(BF16)
                        term = jnp.dot(g_ref[s, l], win, preferred_element_type=F32)
                        acc = term if acc is None else acc + term
                for g in range(groups):
                    for m in range(3):
                        band = None
                        for t in range(BLK):
                            row = (g * BLK + t) * c
                            piece = acc[row : row + c, (t + m) * c : (t + m + 1) * c]
                            band = piece if band is None else band + piece
                        o_ref[i, j, g, m] = band

    return pl.pallas_call(
        kernel, out_shape=jax.ShapeDtypeStruct((layer_taps, 3, groups, 3, c, c), F32)
    )(xu, grad_t)


def banded(weights):
    n_w, _, _, _, c, o = weights.shape
    rows, cols = (BLK + 2) * c, BLK * o

    def kernel(w_ref, o_ref):
        spread = (lax.broadcasted_iota(jnp.int32, (o, cols), 1) % o
                  == lax.broadcasted_iota(jnp.int32, (o, cols), 0)).astype(F32)
        diag = (lax.broadcasted_iota(jnp.int32, (rows, cols), 0) // c
                - lax.broadcasted_iota(jnp.int32, (rows, cols), 1) // o)
        for w in range(n_w):
            for i in range(3):
                for j in range(3):
                    acc = jnp.zeros((rows, cols), F32)
                    for m in range(3):
                        line = jnp.dot(w_ref[w, i, j, m].astype(F32), spread, precision=HIGH,
                                       preferred_element_type=F32)
                        tiled = jnp.broadcast_to(line[None], (BLK + 2, c, cols)).reshape(rows, cols)
                        acc = jnp.where(diag == m, tiled, acc)
                    o_ref[i, j, w] = acc.astype(BF16)

    return pl.pallas_call(
        kernel, out_shape=jax.ShapeDtypeStruct((3, 3, n_w, rows, cols), BF16)
    )(weights)


def tree_sum(x, axes):
    for axis in axes:
        size = lax.axis_size(axis)
        if size & (size - 1):
            x = lax.psum(x, axis)
            continue
        step = 1
        while step < size:
            x = x + lax.ppermute(x, axis, [(i, i ^ step) for i in range(size)])
            step *= 2
    return x


def step(cells, noise, geometry, tile_block, tile_count, w_first, w_second, w_out):
    showers, layer_count, tile_total, channels, _ = cells.shape
    block_total = GR * GP // 128
    slab_count = lax.axis_size("slab")
    lay_count = lax.axis_size("lay")
    nq = GP // BLK
    live_mask = lax.broadcasted_iota(jnp.int32, (layer_count, tile_total), 1) < tile_count[:, None]
    block_ids = lax.broadcasted_iota(jnp.int32, (layer_count, tile_total, block_total), 2)
    onehot = (live_mask[:, :, None] & (tile_block[:, :, None] == block_ids)).astype(F32)
    out_weight = w_out.astype(F32)

    mapped = jnp.einsum("bltcn,ltnp->bltcp", cells, geometry, preferred_element_type=F32)
    grid_sum = jnp.einsum("bltcp,ltk->blkpc", mapped, onehot, precision=HIGH)
    rows = showers * layer_count * GR * nq
    width = BLK * channels
    grid = grid_sum.astype(BF16).reshape(showers, layer_count, GR, nq, width)

    flipped = jnp.swapaxes(jnp.flip(w_second, (0, 1, 2)), 3, 4)
    bands = banded(jnp.stack([w_first, w_second, flipped]))
    grid_u = unfold(layer_halo(grid), channels)
    first = conv_fwd(grid_u, bands[:, :, 0], layer_count)
    first = first.reshape(showers, layer_count, GR, nq, width)
    active = jax.nn.silu(first).astype(BF16)

    active_u = unfold(active, channels)
    second_band = jnp.concatenate([bands[i, :, 1] for i in range(3)], axis=-1)
    parts = conv_fwd(active_u, second_band[None], layer_count).reshape(rows, 3 * width)
    lane = lax.broadcasted_iota(jnp.int32, (3 * width, 3 * BLK), 0)
    slot = lax.broadcasted_iota(jnp.int32, (3 * width, 3 * BLK), 1)
    project = jnp.where(lane // channels == slot, jnp.tile(out_weight, 3 * BLK)[:, None], 0.0)
    projected = jnp.dot(parts, project, precision=HIGH)
    projected = projected.reshape(showers, layer_count, GR, nq, 3, BLK)
    projected = jnp.transpose(projected, (4, 0, 1, 2, 3, 5)).reshape(3, showers, layer_count, GR, GP)
    lower = layer_halo(projected[0])[:, :layer_count]
    upper = layer_halo(projected[2])[:, 2:]
    grid_f = grid.astype(F32).reshape(showers, layer_count, GR, nq, BLK, channels)
    own = jnp.einsum("blrqtc,c->blrqt", grid_f, out_weight, precision=HIGH)
    own = own.reshape(showers, layer_count, GR, GP)
    pred_grid = (own + projected[1] + lower + upper).astype(BF16)

    block_grid = pred_grid.reshape(showers, layer_count, block_total, 128)
    picked = jnp.einsum(
        "blkp,ltk->bltp", block_grid, onehot.astype(BF16), preferred_element_type=F32
    ).astype(BF16)
    predicted = jnp.einsum(
        "bltp,ltnp->bltn", picked, geometry, preferred_element_type=F32
    ).astype(BF16)
    loss_scale = 32.0 / (showers * slab_count * layer_count * lay_count * GR * GP)
    live_f = live_mask.astype(F32)[None, :, :, None]
    cell_grad = (
        (predicted.astype(F32) - noise.astype(F32)) * live_f * loss_scale
    ).astype(BF16)
    back_map = jnp.einsum("bltn,ltnp->bltp", cell_grad, geometry, preferred_element_type=F32)
    grid_grad = jnp.einsum("bltp,ltk->blkp", back_map, onehot, precision=HIGH)
    grid_grad = grid_grad.astype(BF16).reshape(showers, layer_count, GR, nq, BLK)

    grad_h = layer_halo(grid_grad).astype(F32)
    taps_grad = jnp.stack(
        [grad_h[:, 2 - i : 2 - i + layer_count] for i in range(3)], axis=4
    ).reshape(rows, 3 * BLK)
    grad_out = jnp.einsum("blrqtc,blrqt->c", grid_f, grad_h[:, 1 : 1 + layer_count], precision=HIGH)
    weighted = parts.reshape(rows, 3 * BLK, channels) * taps_grad[:, :, None]
    grad_out = grad_out + jnp.sum(weighted, axis=(0, 1))

    second_h = (grad_h[..., None] * out_weight).astype(BF16)
    second_h = second_h.reshape(showers, layer_count + 2, GR, nq, width)
    taps_second = jnp.concatenate(
        [second_h[:, 2 - i : 2 - i + layer_count] for i in range(3)], axis=-1
    ).reshape(showers, layer_count, GR * nq, 3 * width)
    product = conv_wgrad(active_u, jnp.swapaxes(taps_second, 2, 3), 1, channels)
    grad_second = jnp.transpose(product[0], (1, 0, 2, 4, 3))

    early = tree_sum(jnp.concatenate([grad_second.reshape(-1), grad_out]), ("slab", "lay"))
    second_u = unfold(second_h, channels)
    active_grad = conv_fwd(second_u, bands[:, :, 2], layer_count)
    active_grad = active_grad.reshape(showers, layer_count, GR, nq, width)
    sigmoid_z = jax.nn.sigmoid(first)
    first_grad = (active_grad * sigmoid_z * (1.0 + first * (1.0 - sigmoid_z))).astype(BF16)
    first_grad = first_grad.reshape(showers, layer_count, GR * nq, width)
    first_grad_t = jnp.swapaxes(first_grad, 2, 3)
    product = conv_wgrad(grid_u, first_grad_t, 3, channels)
    grad_first = jnp.transpose(product[:, :, 0], (0, 1, 2, 4, 3))

    size = grad_first.size
    grad_first = tree_sum(grad_first.reshape(-1), ("slab", "lay")).reshape(grad_first.shape)
    grad_second = early[:size].reshape(grad_first.shape)
    grad_out = early[size:]
    return (predicted, grad_first, grad_second, grad_out)


def solution(mesh):
    in_specs = (
        P("slab", "lay", None, None, None),
        P("slab", "lay", None, None),
        P("lay", None, None, None),
        P("lay", None),
        P("lay"),
        P(),
        P(),
        P(),
    )
    out_specs = (P("slab", "lay", None, None), P(), P(), P())
    return jax.shard_map(step, mesh=mesh, in_specs=in_specs, out_specs=out_specs, check_vma=False)
```

```python
import jax
import jax.numpy as jnp
from jax import lax
from jax.experimental import pallas as pl
from jax.sharding import PartitionSpec as P


GR = 64
GP = 64
BLK = 8

F32 = jnp.float32
BF16 = jnp.bfloat16
HIGH = lax.Precision.HIGHEST


def layer_halo(x):
    count = lax.axis_size("lay")
    if count == 1:
        zeros = jnp.zeros_like(x[:, :1])
        return jnp.concatenate([zeros, x, zeros], axis=1)
    below = lax.ppermute(x[:, -1:], "lay", [(i, i + 1) for i in range(count - 1)])
    above = lax.ppermute(x[:, :1], "lay", [(i + 1, i) for i in range(count - 1)])
    return jnp.concatenate([below, x, above], axis=1)


def unfold(x, c):
    left = jnp.roll(x[..., (BLK - 1) * c :], 1, axis=3)
    right = jnp.roll(x[..., :c], -1, axis=3)
    full = jnp.concatenate([left, x, right], axis=-1).astype(F32)
    return jnp.pad(full, ((0, 0), (0, 0), (1, 1), (0, 0), (0, 0)))


def conv_fwd(xu, mats, layers):
    s_n, _, rp, q_n, k_n = xu.shape
    t_n, n_n = mats.shape[0], mats.shape[3]
    radial = rp - 2

    def kernel(x_ref, m_ref, o_ref):
        for s in range(s_n):
            for l in range(layers):
                acc = None
                for i in range(t_n):
                    for j in range(3):
                        win = x_ref[s, l + i, j : j + radial].reshape(radial * q_n, k_n).astype(BF16)
                        term = jnp.dot(win, m_ref[i, j], preferred_element_type=F32)
                        acc = term if acc is None else acc + term
                o_ref[s, l] = acc

    return pl.pallas_call(
        kernel, out_shape=jax.ShapeDtypeStruct((s_n, layers, radial * q_n, n_n), F32)
    )(xu, mats)


def conv_wgrad(xu, grad_t, layer_taps, c):
    s_n, _, rp, q_n, k_n = xu.shape
    layers, n_n = grad_t.shape[1], grad_t.shape[2]
    radial = rp - 2
    groups = n_n // (BLK * c)

    def kernel(x_ref, g_ref, o_ref):
        for i in range(layer_taps):
            for j in range(3):
                acc = None
                for s in range(s_n):
                    for l in range(layers):
                        win = x_ref[s, l + i, j : j + radial].reshape(radial * q_n, k_n).astype(BF16)
                        term = jnp.dot(g_ref[s, l], win, preferred_element_type=F32)
                        acc = term if acc is None else acc + term
                for g in range(groups):
                    for m in range(3):
                        band = None
                        for t in range(BLK):
                            row = (g * BLK + t) * c
                            piece = acc[row : row + c, (t + m) * c : (t + m + 1) * c]
                            band = piece if band is None else band + piece
                        o_ref[i, j, g, m] = band

    return pl.pallas_call(
        kernel, out_shape=jax.ShapeDtypeStruct((layer_taps, 3, groups, 3, c, c), F32)
    )(xu, grad_t)


def banded(weights):
    n_w, _, _, _, c, o = weights.shape
    rows, cols = (BLK + 2) * c, BLK * o

    def kernel(w_ref, o_ref):
        spread = (lax.broadcasted_iota(jnp.int32, (o, cols), 1) % o
                  == lax.broadcasted_iota(jnp.int32, (o, cols), 0)).astype(F32)
        diag = (lax.broadcasted_iota(jnp.int32, (rows, cols), 0) // c
                - lax.broadcasted_iota(jnp.int32, (rows, cols), 1) // o)
        for w in range(n_w):
            for i in range(3):
                for j in range(3):
                    acc = jnp.zeros((rows, cols), F32)
                    for m in range(3):
                        line = jnp.dot(w_ref[w, i, j, m].astype(F32), spread, precision=HIGH,
                                       preferred_element_type=F32)
                        tiled = jnp.broadcast_to(line[None], (BLK + 2, c, cols)).reshape(rows, cols)
                        acc = jnp.where(diag == m, tiled, acc)
                    o_ref[i, j, w] = acc.astype(BF16)

    return pl.pallas_call(
        kernel, out_shape=jax.ShapeDtypeStruct((3, 3, n_w, rows, cols), BF16)
    )(weights)


def tree_sum(x, axes):
    for axis in axes:
        size = lax.axis_size(axis)
        if size & (size - 1):
            x = lax.psum(x, axis)
            continue
        step = 1
        while step < size:
            x = x + lax.ppermute(x, axis, [(i, i ^ step) for i in range(size)])
            step *= 2
    return x


def step(cells, noise, geometry, tile_block, tile_count, w_first, w_second, w_out):
    showers, layer_count, tile_total, channels, _ = cells.shape
    block_total = GR * GP // 128
    slab_count = lax.axis_size("slab")
    lay_count = lax.axis_size("lay")
    nq = GP // BLK
    live_mask = lax.broadcasted_iota(jnp.int32, (layer_count, tile_total), 1) < tile_count[:, None]
    block_ids = lax.broadcasted_iota(jnp.int32, (layer_count, tile_total, block_total), 2)
    onehot = (live_mask[:, :, None] & (tile_block[:, :, None] == block_ids)).astype(F32)
    out_weight = w_out.astype(F32)

    mapped = jnp.einsum("bltcn,ltnp->bltcp", cells, geometry, preferred_element_type=F32)
    grid_sum = jnp.einsum("bltcp,ltk->blkpc", mapped, onehot, precision=HIGH)
    rows = showers * layer_count * GR * nq
    width = BLK * channels
    grid = grid_sum.astype(BF16).reshape(showers, layer_count, GR, nq, width)

    flipped = jnp.swapaxes(jnp.flip(w_second, (0, 1, 2)), 3, 4)
    bands = banded(jnp.stack([w_first, w_second, flipped]))
    grid_u = unfold(layer_halo(grid), channels)
    first = conv_fwd(grid_u, bands[:, :, 0], layer_count)
    first = first.reshape(showers, layer_count, GR, nq, width)
    active = jax.nn.silu(first).astype(BF16)

    active_u = unfold(active, channels)
    second_band = jnp.concatenate([bands[i, :, 1] for i in range(3)], axis=-1)
    parts = conv_fwd(active_u, second_band[None], layer_count).reshape(rows, 3 * width)
    lane = lax.broadcasted_iota(jnp.int32, (3 * width, 3 * BLK), 0)
    slot = lax.broadcasted_iota(jnp.int32, (3 * width, 3 * BLK), 1)
    project = jnp.where(lane // channels == slot, jnp.tile(out_weight, 3 * BLK)[:, None], 0.0)
    projected = jnp.dot(parts, project, precision=HIGH)
    projected = projected.reshape(showers, layer_count, GR, nq, 3, BLK)
    projected = jnp.transpose(projected, (4, 0, 1, 2, 3, 5)).reshape(3, showers, layer_count, GR, GP)
    lower = layer_halo(projected[0])[:, :layer_count]
    upper = layer_halo(projected[2])[:, 2:]
    grid_f = grid.astype(F32).reshape(showers, layer_count, GR, nq, BLK, channels)
    own = jnp.einsum("blrqtc,c->blrqt", grid_f, out_weight, precision=HIGH)
    own = own.reshape(showers, layer_count, GR, GP)
    pred_grid = (own + projected[1] + lower + upper).astype(BF16)

    block_grid = pred_grid.reshape(showers, layer_count, block_total, 128)
    picked = jnp.einsum(
        "blkp,ltk->bltp", block_grid, onehot.astype(BF16), preferred_element_type=F32
    ).astype(BF16)
    predicted = jnp.einsum(
        "bltp,ltnp->bltn", picked, geometry, preferred_element_type=F32
    ).astype(BF16)
    loss_scale = 32.0 / (showers * slab_count * layer_count * lay_count * GR * GP)
    live_f = live_mask.astype(F32)[None, :, :, None]
    cell_grad = (
        (predicted.astype(F32) - noise.astype(F32)) * live_f * loss_scale
    ).astype(BF16)
    back_map = jnp.einsum("bltn,ltnp->bltp", cell_grad, geometry, preferred_element_type=F32)
    grid_grad = jnp.einsum("bltp,ltk->blkp", back_map, onehot, precision=HIGH)
    grid_grad = grid_grad.astype(BF16).reshape(showers, layer_count, GR, nq, BLK)

    grad_h = layer_halo(grid_grad)
    taps_grad = jnp.stack(
        [grad_h[:, 2 - i : 2 - i + layer_count] for i in range(3)], axis=4
    ).reshape(rows, 3 * BLK)
    lane = lax.broadcasted_iota(jnp.int32, (3 * BLK, 3 * width), 1)
    slot = lax.broadcasted_iota(jnp.int32, (3 * BLK, 3 * width), 0)
    spread = (lane // channels == slot).astype(BF16)
    taps_wide = jnp.dot(taps_grad, spread, preferred_element_type=F32)
    grad_out = jnp.einsum("blrqtc,blrqt->c", grid_f, grad_h[:, 1 : 1 + layer_count].astype(F32),
                          precision=HIGH)
    weighted = jnp.sum(parts * taps_wide, axis=0).reshape(3 * BLK, channels)
    grad_out = grad_out + jnp.sum(weighted, axis=0)

    lane = lax.broadcasted_iota(jnp.int32, (BLK, width), 1)
    slot = lax.broadcasted_iota(jnp.int32, (BLK, width), 0)
    scale = jnp.where(lane // channels == slot, jnp.tile(w_out, BLK)[None, :], 0).astype(BF16)
    second_h = jnp.dot(grad_h.reshape(-1, BLK), scale, preferred_element_type=F32).astype(BF16)
    second_h = second_h.reshape(showers, layer_count + 2, GR, nq, width)
    taps_second = jnp.concatenate(
        [second_h[:, 2 - i : 2 - i + layer_count] for i in range(3)], axis=-1
    ).reshape(showers, layer_count, GR * nq, 3 * width)
    product = conv_wgrad(active_u, jnp.swapaxes(taps_second, 2, 3), 1, channels)
    grad_second = jnp.transpose(product[0], (1, 0, 2, 4, 3))

    early = tree_sum(jnp.concatenate([grad_second.reshape(-1), grad_out]), ("slab", "lay"))
    second_u = unfold(second_h, channels)
    active_grad = conv_fwd(second_u, bands[:, :, 2], layer_count)
    active_grad = active_grad.reshape(showers, layer_count, GR, nq, width)
    sigmoid_z = jax.nn.sigmoid(first)
    first_grad = (active_grad * sigmoid_z * (1.0 + first * (1.0 - sigmoid_z))).astype(BF16)
    first_grad = first_grad.reshape(showers, layer_count, GR * nq, width)
    first_grad_t = jnp.swapaxes(first_grad, 2, 3)
    product = conv_wgrad(grid_u, first_grad_t, 3, channels)
    grad_first = jnp.transpose(product[:, :, 0], (0, 1, 2, 4, 3))

    size = grad_first.size
    grad_first = tree_sum(grad_first.reshape(-1), ("slab", "lay")).reshape(grad_first.shape)
    grad_second = early[:size].reshape(grad_first.shape)
    grad_out = early[size:]
    return (predicted, grad_first, grad_second, grad_out)


def solution(mesh):
    in_specs = (
        P("slab", "lay", None, None, None),
        P("slab", "lay", None, None),
        P("lay", None, None, None),
        P("lay", None),
        P("lay"),
        P(),
        P(),
        P(),
    )
    out_specs = (P("slab", "lay", None, None), P(), P(), P())
    return jax.shard_map(step, mesh=mesh, in_specs=in_specs, out_specs=out_specs, check_vma=False)
```

```python
import jax
import jax.numpy as jnp
from jax import lax
from jax.experimental import pallas as pl
from jax.sharding import PartitionSpec as P


GR = 64
GP = 64
BLK = 8

F32 = jnp.float32
BF16 = jnp.bfloat16
HIGH = lax.Precision.HIGHEST


def layer_halo(x):
    count = lax.axis_size("lay")
    if count == 1:
        zeros = jnp.zeros_like(x[:, :1])
        return jnp.concatenate([zeros, x, zeros], axis=1)
    below = lax.ppermute(x[:, -1:], "lay", [(i, i + 1) for i in range(count - 1)])
    above = lax.ppermute(x[:, :1], "lay", [(i + 1, i) for i in range(count - 1)])
    return jnp.concatenate([below, x, above], axis=1)


def unfold(x, c):
    left = jnp.roll(x[..., (BLK - 1) * c :], 1, axis=3)
    right = jnp.roll(x[..., :c], -1, axis=3)
    full = jnp.concatenate([left, x, right], axis=-1).astype(F32)
    return jnp.pad(full, ((0, 0), (0, 0), (1, 1), (0, 0), (0, 0)))


def conv_fwd(xu, mats, layers):
    s_n, _, rp, q_n, k_n = xu.shape
    t_n, n_n = mats.shape[0], mats.shape[3]
    radial = rp - 2

    def kernel(x_ref, m_ref, o_ref):
        for s in range(s_n):
            for l in range(layers):
                acc = None
                for i in range(t_n):
                    for j in range(3):
                        win = x_ref[s, l + i, j : j + radial].reshape(radial * q_n, k_n).astype(BF16)
                        term = jnp.dot(win, m_ref[i, j], preferred_element_type=F32)
                        acc = term if acc is None else acc + term
                o_ref[s, l] = acc

    return pl.pallas_call(
        kernel, out_shape=jax.ShapeDtypeStruct((s_n, layers, radial * q_n, n_n), F32)
    )(xu, mats)


def conv_wgrad(xu, grad_t, layer_taps, c):
    s_n, _, rp, q_n, k_n = xu.shape
    layers, n_n = grad_t.shape[1], grad_t.shape[2]
    radial = rp - 2
    groups = n_n // (BLK * c)

    def kernel(x_ref, g_ref, o_ref):
        for i in range(layer_taps):
            for j in range(3):
                acc = None
                for s in range(s_n):
                    for l in range(layers):
                        win = x_ref[s, l + i, j : j + radial].reshape(radial * q_n, k_n).astype(BF16)
                        term = jnp.dot(g_ref[s, l], win, preferred_element_type=F32)
                        acc = term if acc is None else acc + term
                for g in range(groups):
                    for m in range(3):
                        band = None
                        for t in range(BLK):
                            row = (g * BLK + t) * c
                            piece = acc[row : row + c, (t + m) * c : (t + m + 1) * c]
                            band = piece if band is None else band + piece
                        o_ref[i, j, g, m] = band

    return pl.pallas_call(
        kernel, out_shape=jax.ShapeDtypeStruct((layer_taps, 3, groups, 3, c, c), F32)
    )(xu, grad_t)


def banded(weights):
    n_w, _, _, _, c, o = weights.shape
    rows, cols = (BLK + 2) * c, BLK * o

    def kernel(w_ref, o_ref):
        spread = (lax.broadcasted_iota(jnp.int32, (o, cols), 1) % o
                  == lax.broadcasted_iota(jnp.int32, (o, cols), 0)).astype(F32)
        diag = (lax.broadcasted_iota(jnp.int32, (rows, cols), 0) // c
                - lax.broadcasted_iota(jnp.int32, (rows, cols), 1) // o)
        for w in range(n_w):
            for i in range(3):
                for j in range(3):
                    acc = jnp.zeros((rows, cols), F32)
                    for m in range(3):
                        line = jnp.dot(w_ref[w, i, j, m].astype(F32), spread, precision=HIGH,
                                       preferred_element_type=F32)
                        tiled = jnp.broadcast_to(line[None], (BLK + 2, c, cols)).reshape(rows, cols)
                        acc = jnp.where(diag == m, tiled, acc)
                    o_ref[i, j, w] = acc.astype(BF16)

    return pl.pallas_call(
        kernel, out_shape=jax.ShapeDtypeStruct((3, 3, n_w, rows, cols), BF16)
    )(weights)


def tree_sum(x, axes):
    for axis in axes:
        size = lax.axis_size(axis)
        if size & (size - 1):
            x = lax.psum(x, axis)
            continue
        bit = 1
        while bit < size:
            peer = lambda flip: lax.ppermute(x, axis, [(i, i ^ flip) for i in range(size)])
            if bit * 2 < size:
                x = (x + peer(bit)) + (peer(bit * 2) + peer(bit * 3))
                bit *= 4
            else:
                x = x + peer(bit)
                bit *= 2
    return x


def step(cells, noise, geometry, tile_block, tile_count, w_first, w_second, w_out):
    showers, layer_count, tile_total, channels, _ = cells.shape
    block_total = GR * GP // 128
    slab_count = lax.axis_size("slab")
    lay_count = lax.axis_size("lay")
    nq = GP // BLK
    live_mask = lax.broadcasted_iota(jnp.int32, (layer_count, tile_total), 1) < tile_count[:, None]
    block_ids = lax.broadcasted_iota(jnp.int32, (layer_count, tile_total, block_total), 2)
    onehot = (live_mask[:, :, None] & (tile_block[:, :, None] == block_ids)).astype(F32)
    out_weight = w_out.astype(F32)

    mapped = jnp.einsum("bltcn,ltnp->bltcp", cells, geometry, preferred_element_type=F32)
    grid_sum = jnp.einsum("bltcp,ltk->blkpc", mapped, onehot, precision=HIGH)
    rows = showers * layer_count * GR * nq
    width = BLK * channels
    grid = grid_sum.astype(BF16).reshape(showers, layer_count, GR, nq, width)

    flipped = jnp.swapaxes(jnp.flip(w_second, (0, 1, 2)), 3, 4)
    bands = banded(jnp.stack([w_first, w_second, flipped]))
    grid_u = unfold(layer_halo(grid), channels)
    first = conv_fwd(grid_u, bands[:, :, 0], layer_count)
    first = first.reshape(showers, layer_count, GR, nq, width)
    active = jax.nn.silu(first).astype(BF16)

    active_u = unfold(active, channels)
    second_band = jnp.concatenate([bands[i, :, 1] for i in range(3)], axis=-1)
    parts = conv_fwd(active_u, second_band[None], layer_count).reshape(rows, 3 * width)
    lane = lax.broadcasted_iota(jnp.int32, (3 * width, 3 * BLK), 0)
    slot = lax.broadcasted_iota(jnp.int32, (3 * width, 3 * BLK), 1)
    project = jnp.where(lane // channels == slot, jnp.tile(out_weight, 3 * BLK)[:, None], 0.0)
    projected = jnp.dot(parts, project, precision=HIGH)
    projected = projected.reshape(showers, layer_count, GR, nq, 3, BLK)
    projected = jnp.transpose(projected, (4, 0, 1, 2, 3, 5)).reshape(3, showers, layer_count, GR, GP)
    lower = layer_halo(projected[0])[:, :layer_count]
    upper = layer_halo(projected[2])[:, 2:]
    grid_f = grid.astype(F32).reshape(showers, layer_count, GR, nq, BLK, channels)
    own = jnp.einsum("blrqtc,c->blrqt", grid_f, out_weight, precision=HIGH)
    own = own.reshape(showers, layer_count, GR, GP)
    pred_grid = (own + projected[1] + lower + upper).astype(BF16)

    block_grid = pred_grid.reshape(showers, layer_count, block_total, 128)
    picked = jnp.einsum(
        "blkp,ltk->bltp", block_grid, onehot.astype(BF16), preferred_element_type=F32
    ).astype(BF16)
    predicted = jnp.einsum(
        "bltp,ltnp->bltn", picked, geometry, preferred_element_type=F32
    ).astype(BF16)
    loss_scale = 32.0 / (showers * slab_count * layer_count * lay_count * GR * GP)
    live_f = live_mask.astype(F32)[None, :, :, None]
    cell_grad = (
        (predicted.astype(F32) - noise.astype(F32)) * live_f * loss_scale
    ).astype(BF16)
    back_map = jnp.einsum("bltn,ltnp->bltp", cell_grad, geometry, preferred_element_type=F32)
    grid_grad = jnp.einsum("bltp,ltk->blkp", back_map, onehot, precision=HIGH)
    grid_grad = grid_grad.astype(BF16).reshape(showers, layer_count, GR, nq, BLK)

    grad_h = layer_halo(grid_grad)
    taps_grad = jnp.stack(
        [grad_h[:, 2 - i : 2 - i + layer_count] for i in range(3)], axis=4
    ).reshape(rows, 3 * BLK)
    lane = lax.broadcasted_iota(jnp.int32, (3 * BLK, 3 * width), 1)
    slot = lax.broadcasted_iota(jnp.int32, (3 * BLK, 3 * width), 0)
    spread = (lane // channels == slot).astype(BF16)
    taps_wide = jnp.dot(taps_grad, spread, preferred_element_type=F32)
    grad_out = jnp.einsum("blrqtc,blrqt->c", grid_f, grad_h[:, 1 : 1 + layer_count].astype(F32),
                          precision=HIGH)
    weighted = jnp.sum(parts * taps_wide, axis=0).reshape(3 * BLK, channels)
    grad_out = grad_out + jnp.sum(weighted, axis=0)

    lane = lax.broadcasted_iota(jnp.int32, (BLK, width), 1)
    slot = lax.broadcasted_iota(jnp.int32, (BLK, width), 0)
    scale = jnp.where(lane // channels == slot, jnp.tile(w_out, BLK)[None, :], 0).astype(BF16)
    second_h = jnp.dot(grad_h.reshape(-1, BLK), scale, preferred_element_type=F32).astype(BF16)
    second_h = second_h.reshape(showers, layer_count + 2, GR, nq, width)
    taps_second = jnp.concatenate(
        [second_h[:, 2 - i : 2 - i + layer_count] for i in range(3)], axis=-1
    ).reshape(showers, layer_count, GR * nq, 3 * width)
    product = conv_wgrad(active_u, jnp.swapaxes(taps_second, 2, 3), 1, channels)
    grad_second = jnp.transpose(product[0], (1, 0, 2, 4, 3))

    early = tree_sum(jnp.concatenate([grad_second.reshape(-1), grad_out]), ("slab", "lay"))
    second_u = unfold(second_h, channels)
    active_grad = conv_fwd(second_u, bands[:, :, 2], layer_count)
    active_grad = active_grad.reshape(showers, layer_count, GR, nq, width)
    sigmoid_z = jax.nn.sigmoid(first)
    first_grad = (active_grad * sigmoid_z * (1.0 + first * (1.0 - sigmoid_z))).astype(BF16)
    first_grad = first_grad.reshape(showers, layer_count, GR * nq, width)
    first_grad_t = jnp.swapaxes(first_grad, 2, 3)
    product = conv_wgrad(grid_u, first_grad_t, 3, channels)
    grad_first = jnp.transpose(product[:, :, 0], (0, 1, 2, 4, 3))

    size = grad_first.size
    grad_first = tree_sum(grad_first.reshape(-1), ("slab", "lay")).reshape(grad_first.shape)
    grad_second = early[:size].reshape(grad_first.shape)
    grad_out = early[size:]
    return (predicted, grad_first, grad_second, grad_out)


def solution(mesh):
    in_specs = (
        P("slab", "lay", None, None, None),
        P("slab", "lay", None, None),
        P("lay", None, None, None),
        P("lay", None),
        P("lay"),
        P(),
        P(),
        P(),
    )
    out_specs = (P("slab", "lay", None, None), P(), P(), P())
    return jax.shard_map(step, mesh=mesh, in_specs=in_specs, out_specs=out_specs, check_vma=False)
```

```python
import jax
import jax.numpy as jnp
from jax import lax
from jax.experimental import pallas as pl
from jax.sharding import PartitionSpec as P


GR = 64
GP = 64
BLK = 8

F32 = jnp.float32
BF16 = jnp.bfloat16
HIGH = lax.Precision.HIGHEST


def layer_halo(x):
    count = lax.axis_size("lay")
    if count == 1:
        zeros = jnp.zeros_like(x[:, :1])
        return jnp.concatenate([zeros, x, zeros], axis=1)
    below = lax.ppermute(x[:, -1:], "lay", [(i, i + 1) for i in range(count - 1)])
    above = lax.ppermute(x[:, :1], "lay", [(i + 1, i) for i in range(count - 1)])
    return jnp.concatenate([below, x, above], axis=1)


def unfold(x, c):
    left = jnp.roll(x[..., (BLK - 1) * c :], 1, axis=3)
    right = jnp.roll(x[..., :c], -1, axis=3)
    full = jnp.concatenate([left, x, right], axis=-1).astype(F32)
    return jnp.pad(full, ((0, 0), (0, 0), (1, 1), (0, 0), (0, 0)))


def conv_fwd(xu, mats, layers):
    s_n, _, rp, q_n, k_n = xu.shape
    t_n, n_n = mats.shape[0], mats.shape[3]
    radial = rp - 2

    def kernel(x_ref, m_ref, o_ref):
        for s in range(s_n):
            for l in range(layers):
                acc = None
                for i in range(t_n):
                    for j in range(3):
                        win = x_ref[s, l + i, j : j + radial].reshape(radial * q_n, k_n).astype(BF16)
                        term = jnp.dot(win, m_ref[i, j], preferred_element_type=F32)
                        acc = term if acc is None else acc + term
                o_ref[s, l] = acc

    return pl.pallas_call(
        kernel, out_shape=jax.ShapeDtypeStruct((s_n, layers, radial * q_n, n_n), F32)
    )(xu, mats)


def conv_wgrad(xu, grad_t, layer_taps, c):
    s_n, _, rp, q_n, k_n = xu.shape
    layers, n_n = grad_t.shape[1], grad_t.shape[2]
    radial = rp - 2
    groups = n_n // (BLK * c)

    def kernel(x_ref, g_ref, o_ref):
        for i in range(layer_taps):
            for j in range(3):
                acc = None
                for s in range(s_n):
                    for l in range(layers):
                        win = x_ref[s, l + i, j : j + radial].reshape(radial * q_n, k_n).astype(BF16)
                        term = jnp.dot(g_ref[s, l], win, preferred_element_type=F32)
                        acc = term if acc is None else acc + term
                for g in range(groups):
                    for m in range(3):
                        band = None
                        for t in range(BLK):
                            row = (g * BLK + t) * c
                            piece = acc[row : row + c, (t + m) * c : (t + m + 1) * c]
                            band = piece if band is None else band + piece
                        o_ref[i, j, g, m] = band

    return pl.pallas_call(
        kernel, out_shape=jax.ShapeDtypeStruct((layer_taps, 3, groups, 3, c, c), F32)
    )(xu, grad_t)


def banded(weights):
    n_w, _, _, _, c, o = weights.shape
    rows, cols = (BLK + 2) * c, BLK * o

    def kernel(w_ref, o_ref):
        spread = (lax.broadcasted_iota(jnp.int32, (o, cols), 1) % o
                  == lax.broadcasted_iota(jnp.int32, (o, cols), 0)).astype(F32)
        diag = (lax.broadcasted_iota(jnp.int32, (rows, cols), 0) // c
                - lax.broadcasted_iota(jnp.int32, (rows, cols), 1) // o)
        for w in range(n_w):
            for i in range(3):
                for j in range(3):
                    acc = jnp.zeros((rows, cols), F32)
                    for m in range(3):
                        line = jnp.dot(w_ref[w, i, j, m].astype(F32), spread, precision=HIGH,
                                       preferred_element_type=F32)
                        tiled = jnp.broadcast_to(line[None], (BLK + 2, c, cols)).reshape(rows, cols)
                        acc = jnp.where(diag == m, tiled, acc)
                    o_ref[i, j, w] = acc.astype(BF16)

    return pl.pallas_call(
        kernel, out_shape=jax.ShapeDtypeStruct((3, 3, n_w, rows, cols), BF16)
    )(weights)


def tree_sum(x, axes):
    for axis in axes:
        size = lax.axis_size(axis)
        if size & (size - 1):
            x = lax.psum(x, axis)
            continue
        bit = 1
        while bit < size:
            peer = lambda flip: lax.ppermute(x, axis, [(i, i ^ flip) for i in range(size)])
            if bit * 2 < size:
                x = (x + peer(bit)) + (peer(bit * 2) + peer(bit * 3))
                bit *= 4
            else:
                x = x + peer(bit)
                bit *= 2
    return x


def step(cells, noise, geometry, tile_block, tile_count, w_first, w_second, w_out):
    showers, layer_count, tile_total, channels, _ = cells.shape
    block_total = GR * GP // 128
    slab_count = lax.axis_size("slab")
    lay_count = lax.axis_size("lay")
    nq = GP // BLK
    live_mask = lax.broadcasted_iota(jnp.int32, (layer_count, tile_total), 1) < tile_count[:, None]
    block_ids = lax.broadcasted_iota(jnp.int32, (layer_count, tile_total, block_total), 2)
    onehot = (live_mask[:, :, None] & (tile_block[:, :, None] == block_ids)).astype(F32)
    out_weight = w_out.astype(F32)

    mapped = jnp.einsum("bltcn,ltnp->bltcp", cells, geometry, preferred_element_type=F32)
    grid_sum = jnp.einsum("bltcp,ltk->blkpc", mapped, onehot, precision=HIGH)
    rows = showers * layer_count * GR * nq
    width = BLK * channels
    grid = grid_sum.astype(BF16).reshape(showers, layer_count, GR, nq, width)

    flipped = jnp.swapaxes(jnp.flip(w_second, (0, 1, 2)), 3, 4)
    bands = banded(jnp.stack([w_first, w_second, flipped]))
    grid_u = unfold(layer_halo(grid), channels)
    first = conv_fwd(grid_u, bands[:, :, 0], layer_count)
    first = first.reshape(showers, layer_count, GR, nq, width)
    active = jax.nn.silu(first).astype(BF16)

    active_u = unfold(active, channels)
    second_band = jnp.concatenate([bands[i, :, 1] for i in range(3)], axis=-1)
    parts = conv_fwd(active_u, second_band[None], layer_count).reshape(rows, 3 * width)
    lane = lax.broadcasted_iota(jnp.int32, (3 * width, 3 * BLK), 0)
    slot = lax.broadcasted_iota(jnp.int32, (3 * width, 3 * BLK), 1)
    project = jnp.where(lane // channels == slot, jnp.tile(out_weight, 3 * BLK)[:, None], 0.0)
    projected = jnp.dot(parts, project, precision=HIGH)
    projected = projected.reshape(showers, layer_count, GR, nq, 3, BLK)
    projected = jnp.transpose(projected, (4, 0, 1, 2, 3, 5)).reshape(3, showers, layer_count, GR, GP)
    lower = layer_halo(projected[0])[:, :layer_count]
    upper = layer_halo(projected[2])[:, 2:]
    grid_f = grid.astype(F32).reshape(showers, layer_count, GR, nq, BLK, channels)
    own = jnp.einsum("blrqtc,c->blrqt", grid_f, out_weight, precision=HIGH)
    own = own.reshape(showers, layer_count, GR, GP)
    pred_grid = (own + projected[1] + lower + upper).astype(BF16)

    block_grid = pred_grid.reshape(showers, layer_count, block_total, 128)
    picked = jnp.einsum(
        "blkp,ltk->bltp", block_grid, onehot.astype(BF16), preferred_element_type=F32
    ).astype(BF16)
    predicted = jnp.einsum(
        "bltp,ltnp->bltn", picked, geometry, preferred_element_type=F32
    ).astype(BF16)
    loss_scale = 32.0 / (showers * slab_count * layer_count * lay_count * GR * GP)
    live_f = live_mask.astype(F32)[None, :, :, None]
    cell_grad = (
        (predicted.astype(F32) - noise.astype(F32)) * live_f * loss_scale
    ).astype(BF16)
    back_map = jnp.einsum("bltn,ltnp->bltp", cell_grad, geometry, preferred_element_type=F32)
    grid_grad = jnp.einsum("bltp,ltk->blkp", back_map, onehot, precision=HIGH)
    grid_grad = grid_grad.astype(BF16).reshape(showers, layer_count, GR, nq, BLK)

    grad_h = layer_halo(grid_grad)
    taps_grad = jnp.stack(
        [grad_h[:, 2 - i : 2 - i + layer_count] for i in range(3)], axis=4
    ).reshape(rows, 3 * BLK)
    lane = lax.broadcasted_iota(jnp.int32, (3 * BLK, 3 * width), 1)
    slot = lax.broadcasted_iota(jnp.int32, (3 * BLK, 3 * width), 0)
    spread = (lane // channels == slot).astype(BF16)
    taps_wide = jnp.dot(taps_grad, spread, preferred_element_type=F32)
    grad_out = jnp.einsum("blrqtc,blrqt->c", grid_f, grad_h[:, 1 : 1 + layer_count].astype(F32),
                          precision=HIGH)
    weighted = jnp.sum(parts * taps_wide, axis=0).reshape(3 * BLK, channels)
    grad_out = grad_out + jnp.sum(weighted, axis=0)

    lane = lax.broadcasted_iota(jnp.int32, (BLK, width), 1)
    slot = lax.broadcasted_iota(jnp.int32, (BLK, width), 0)
    scale = jnp.where(lane // channels == slot, jnp.tile(w_out, BLK)[None, :], 0).astype(BF16)
    second_h = jnp.dot(grad_h.reshape(-1, BLK), scale, preferred_element_type=F32).astype(BF16)
    second_h = second_h.reshape(showers, layer_count + 2, GR, nq, width)
    taps_second = jnp.concatenate(
        [second_h[:, 2 - i : 2 - i + layer_count] for i in range(3)], axis=-1
    ).reshape(showers, layer_count, GR * nq, 3 * width)
    product = conv_wgrad(active_u, jnp.swapaxes(taps_second, 2, 3), 1, channels)
    grad_second = jnp.transpose(product[0], (1, 0, 2, 4, 3))

    early = tree_sum(jnp.concatenate([grad_second.reshape(-1), grad_out]), ("slab",))
    second_u = unfold(second_h, channels)
    active_grad = conv_fwd(second_u, bands[:, :, 2], layer_count)
    active_grad = active_grad.reshape(showers, layer_count, GR, nq, width)
    sigmoid_z = jax.nn.sigmoid(first)
    first_grad = (active_grad * sigmoid_z * (1.0 + first * (1.0 - sigmoid_z))).astype(BF16)
    first_grad = first_grad.reshape(showers, layer_count, GR * nq, width)
    first_grad_t = jnp.swapaxes(first_grad, 2, 3)
    product = conv_wgrad(grid_u, first_grad_t, 3, channels)
    grad_first = jnp.transpose(product[:, :, 0], (0, 1, 2, 4, 3))

    size = grad_first.size
    late = tree_sum(grad_first.reshape(-1), ("slab",))
    both = tree_sum(jnp.concatenate([late, early]), ("lay",))
    grad_first = both[:size].reshape(grad_first.shape)
    grad_second = both[size : 2 * size].reshape(grad_first.shape)
    grad_out = both[2 * size :]
    return (predicted, grad_first, grad_second, grad_out)


def solution(mesh):
    in_specs = (
        P("slab", "lay", None, None, None),
        P("slab", "lay", None, None),
        P("lay", None, None, None),
        P("lay", None),
        P("lay"),
        P(),
        P(),
        P(),
    )
    out_specs = (P("slab", "lay", None, None), P(), P(), P())
    return jax.shard_map(step, mesh=mesh, in_specs=in_specs, out_specs=out_specs, check_vma=False)
```

```python
import jax
import jax.numpy as jnp
from jax import lax
from jax.experimental import pallas as pl
from jax.sharding import PartitionSpec as P


GR = 64
GP = 64
BLK = 8

F32 = jnp.float32
BF16 = jnp.bfloat16
HIGH = lax.Precision.HIGHEST


def layer_halo(x):
    count = lax.axis_size("lay")
    if count == 1:
        zeros = jnp.zeros_like(x[:, :1])
        return jnp.concatenate([zeros, x, zeros], axis=1)
    below = lax.ppermute(x[:, -1:], "lay", [(i, i + 1) for i in range(count - 1)])
    above = lax.ppermute(x[:, :1], "lay", [(i + 1, i) for i in range(count - 1)])
    return jnp.concatenate([below, x, above], axis=1)


def unfold(x, c):
    left = jnp.roll(x[..., (BLK - 1) * c :], 1, axis=3)
    right = jnp.roll(x[..., :c], -1, axis=3)
    full = jnp.concatenate([left, x, right], axis=-1).astype(F32)
    return jnp.pad(full, ((0, 0), (0, 0), (1, 1), (0, 0), (0, 0)))


def conv_fwd(xu, mats, layers):
    s_n, _, rp, q_n, k_n = xu.shape
    t_n, n_n = mats.shape[0], mats.shape[3]
    radial = rp - 2

    def kernel(x_ref, m_ref, o_ref):
        for s in range(s_n):
            for l in range(layers):
                acc = None
                for i in range(t_n):
                    for j in range(3):
                        win = x_ref[s, l + i, j : j + radial].reshape(radial * q_n, k_n).astype(BF16)
                        term = jnp.dot(win, m_ref[i, j], preferred_element_type=F32)
                        acc = term if acc is None else acc + term
                o_ref[s, l] = acc

    return pl.pallas_call(
        kernel, out_shape=jax.ShapeDtypeStruct((s_n, layers, radial * q_n, n_n), F32)
    )(xu, mats)


def conv_wgrad(xu, grad_t, layer_taps, c):
    s_n, _, rp, q_n, k_n = xu.shape
    layers, n_n = grad_t.shape[1], grad_t.shape[2]
    radial = rp - 2
    groups = n_n // (BLK * c)

    def kernel(x_ref, g_ref, o_ref):
        for i in range(layer_taps):
            for j in range(3):
                acc = None
                for s in range(s_n):
                    for l in range(layers):
                        win = x_ref[s, l + i, j : j + radial].reshape(radial * q_n, k_n).astype(BF16)
                        term = jnp.dot(g_ref[s, l], win, preferred_element_type=F32)
                        acc = term if acc is None else acc + term
                for g in range(groups):
                    for m in range(3):
                        band = None
                        for t in range(BLK):
                            row = (g * BLK + t) * c
                            piece = acc[row : row + c, (t + m) * c : (t + m + 1) * c]
                            band = piece if band is None else band + piece
                        o_ref[i, j, g, m] = band

    return pl.pallas_call(
        kernel, out_shape=jax.ShapeDtypeStruct((layer_taps, 3, groups, 3, c, c), F32)
    )(xu, grad_t)


def banded(weights):
    n_w, _, _, _, c, o = weights.shape
    rows, cols = (BLK + 2) * c, BLK * o

    def kernel(w_ref, o_ref):
        spread = (lax.broadcasted_iota(jnp.int32, (o, cols), 1) % o
                  == lax.broadcasted_iota(jnp.int32, (o, cols), 0)).astype(F32)
        diag = (lax.broadcasted_iota(jnp.int32, (rows, cols), 0) // c
                - lax.broadcasted_iota(jnp.int32, (rows, cols), 1) // o)
        for w in range(n_w):
            for i in range(3):
                for j in range(3):
                    acc = jnp.zeros((rows, cols), F32)
                    for m in range(3):
                        line = jnp.dot(w_ref[w, i, j, m].astype(F32), spread, precision=HIGH,
                                       preferred_element_type=F32)
                        tiled = jnp.broadcast_to(line[None], (BLK + 2, c, cols)).reshape(rows, cols)
                        acc = jnp.where(diag == m, tiled, acc)
                    o_ref[i, j, w] = acc.astype(BF16)

    return pl.pallas_call(
        kernel, out_shape=jax.ShapeDtypeStruct((3, 3, n_w, rows, cols), BF16)
    )(weights)


def tree_sum(x, axes):
    for axis in axes:
        size = lax.axis_size(axis)
        if size & (size - 1):
            x = lax.psum(x, axis)
            continue
        bit = 1
        while bit < size:
            span = 1
            while span < 8 and bit * span * 2 <= size:
                span *= 2
            vals = [x] + [lax.ppermute(x, axis, [(i, i ^ (f * bit)) for i in range(size)])
                          for f in range(1, span)]
            while len(vals) > 1:
                vals = [vals[k] + vals[k + 1] for k in range(0, len(vals), 2)]
            x = vals[0]
            bit *= span
    return x


def step(cells, noise, geometry, tile_block, tile_count, w_first, w_second, w_out):
    showers, layer_count, tile_total, channels, _ = cells.shape
    block_total = GR * GP // 128
    slab_count = lax.axis_size("slab")
    lay_count = lax.axis_size("lay")
    nq = GP // BLK
    live_mask = lax.broadcasted_iota(jnp.int32, (layer_count, tile_total), 1) < tile_count[:, None]
    block_ids = lax.broadcasted_iota(jnp.int32, (layer_count, tile_total, block_total), 2)
    onehot = (live_mask[:, :, None] & (tile_block[:, :, None] == block_ids)).astype(F32)
    out_weight = w_out.astype(F32)

    mapped = jnp.einsum("bltcn,ltnp->bltcp", cells, geometry, preferred_element_type=F32)
    grid_sum = jnp.einsum("bltcp,ltk->blkpc", mapped, onehot, precision=HIGH)
    rows = showers * layer_count * GR * nq
    width = BLK * channels
    grid = grid_sum.astype(BF16).reshape(showers, layer_count, GR, nq, width)

    flipped = jnp.swapaxes(jnp.flip(w_second, (0, 1, 2)), 3, 4)
    bands = banded(jnp.stack([w_first, w_second, flipped]))
    grid_u = unfold(layer_halo(grid), channels)
    first = conv_fwd(grid_u, bands[:, :, 0], layer_count)
    first = first.reshape(showers, layer_count, GR, nq, width)
    active = jax.nn.silu(first).astype(BF16)

    active_u = unfold(active, channels)
    second_band = jnp.concatenate([bands[i, :, 1] for i in range(3)], axis=-1)
    parts = conv_fwd(active_u, second_band[None], layer_count).reshape(rows, 3 * width)
    lane = lax.broadcasted_iota(jnp.int32, (3 * width, 3 * BLK), 0)
    slot = lax.broadcasted_iota(jnp.int32, (3 * width, 3 * BLK), 1)
    project = jnp.where(lane // channels == slot, jnp.tile(out_weight, 3 * BLK)[:, None], 0.0)
    projected = jnp.dot(parts, project, precision=HIGH)
    projected = projected.reshape(showers, layer_count, GR, nq, 3, BLK)
    projected = jnp.transpose(projected, (4, 0, 1, 2, 3, 5)).reshape(3, showers, layer_count, GR, GP)
    lower = layer_halo(projected[0])[:, :layer_count]
    upper = layer_halo(projected[2])[:, 2:]
    grid_f = grid.astype(F32).reshape(showers, layer_count, GR, nq, BLK, channels)
    own = jnp.einsum("blrqtc,c->blrqt", grid_f, out_weight, precision=HIGH)
    own = own.reshape(showers, layer_count, GR, GP)
    pred_grid = (own + projected[1] + lower + upper).astype(BF16)

    block_grid = pred_grid.reshape(showers, layer_count, block_total, 128)
    picked = jnp.einsum(
        "blkp,ltk->bltp", block_grid, onehot.astype(BF16), preferred_element_type=F32
    ).astype(BF16)
    predicted = jnp.einsum(
        "bltp,ltnp->bltn", picked, geometry, preferred_element_type=F32
    ).astype(BF16)
    loss_scale = 32.0 / (showers * slab_count * layer_count * lay_count * GR * GP)
    live_f = live_mask.astype(F32)[None, :, :, None]
    cell_grad = (
        (predicted.astype(F32) - noise.astype(F32)) * live_f * loss_scale
    ).astype(BF16)
    back_map = jnp.einsum("bltn,ltnp->bltp", cell_grad, geometry, preferred_element_type=F32)
    grid_grad = jnp.einsum("bltp,ltk->blkp", back_map, onehot, precision=HIGH)
    grid_grad = grid_grad.astype(BF16).reshape(showers, layer_count, GR, nq, BLK)

    grad_h = layer_halo(grid_grad)
    taps_grad = jnp.stack(
        [grad_h[:, 2 - i : 2 - i + layer_count] for i in range(3)], axis=4
    ).reshape(rows, 3 * BLK)
    lane = lax.broadcasted_iota(jnp.int32, (3 * BLK, 3 * width), 1)
    slot = lax.broadcasted_iota(jnp.int32, (3 * BLK, 3 * width), 0)
    spread = (lane // channels == slot).astype(BF16)
    taps_wide = jnp.dot(taps_grad, spread, preferred_element_type=F32)
    grad_out = jnp.einsum("blrqtc,blrqt->c", grid_f, grad_h[:, 1 : 1 + layer_count].astype(F32),
                          precision=HIGH)
    weighted = jnp.sum(parts * taps_wide, axis=0).reshape(3 * BLK, channels)
    grad_out = grad_out + jnp.sum(weighted, axis=0)

    lane = lax.broadcasted_iota(jnp.int32, (BLK, width), 1)
    slot = lax.broadcasted_iota(jnp.int32, (BLK, width), 0)
    scale = jnp.where(lane // channels == slot, jnp.tile(w_out, BLK)[None, :], 0).astype(BF16)
    second_h = jnp.dot(grad_h.reshape(-1, BLK), scale, preferred_element_type=F32).astype(BF16)
    second_h = second_h.reshape(showers, layer_count + 2, GR, nq, width)
    taps_second = jnp.concatenate(
        [second_h[:, 2 - i : 2 - i + layer_count] for i in range(3)], axis=-1
    ).reshape(showers, layer_count, GR * nq, 3 * width)
    product = conv_wgrad(active_u, jnp.swapaxes(taps_second, 2, 3), 1, channels)
    grad_second = jnp.transpose(product[0], (1, 0, 2, 4, 3))

    early = tree_sum(jnp.concatenate([grad_second.reshape(-1), grad_out]), ("slab", "lay"))
    second_u = unfold(second_h, channels)
    active_grad = conv_fwd(second_u, bands[:, :, 2], layer_count)
    active_grad = active_grad.reshape(showers, layer_count, GR, nq, width)
    sigmoid_z = jax.nn.sigmoid(first)
    first_grad = (active_grad * sigmoid_z * (1.0 + first * (1.0 - sigmoid_z))).astype(BF16)
    first_grad = first_grad.reshape(showers, layer_count, GR * nq, width)
    first_grad_t = jnp.swapaxes(first_grad, 2, 3)
    product = conv_wgrad(grid_u, first_grad_t, 3, channels)
    grad_first = jnp.transpose(product[:, :, 0], (0, 1, 2, 4, 3))

    size = grad_first.size
    grad_first = tree_sum(grad_first.reshape(-1), ("slab", "lay")).reshape(grad_first.shape)
    grad_second = early[:size].reshape(grad_first.shape)
    grad_out = early[size:]
    return (predicted, grad_first, grad_second, grad_out)


def solution(mesh):
    in_specs = (
        P("slab", "lay", None, None, None),
        P("slab", "lay", None, None),
        P("lay", None, None, None),
        P("lay", None),
        P("lay"),
        P(),
        P(),
        P(),
    )
    out_specs = (P("slab", "lay", None, None), P(), P(), P())
    return jax.shard_map(step, mesh=mesh, in_specs=in_specs, out_specs=out_specs, check_vma=False)
```
